32 devices in a mesh: groups: 2 (over x), tile: 16 (over z, y, core).
Axes of the slice: x: 2, y: 2, z: 4, core: 2. Of those that a mesh axis runs over, the one named last changes fastest.
Arguments:
- hidden_in: bfloat16 [2048, 4096], P('groups', 'tile'), parts along dimension 0, may hold values from -6 to 6
- w_up: bfloat16 [16, 1024, 4096], P('tile'), may hold values from -0.09375 to 0.09375
- w_down: bfloat16 [16, 4096, 1024], P('tile'), may hold values from -0.046875 to 0.046875
- out_grad: bfloat16 [2048, 4096], P('groups', 'tile'), parts along dimension 0, may hold values from -6 to 6
Outputs:
- block_out: bfloat16 [2048, 4096], P('groups', 'tile'), parts along dimension 0
- input_grad: bfloat16 [2048, 4096], P('groups', 'tile'), parts along dimension 0
- grad_up: bfloat16 [16, 2048, 4096], P('tile', 'groups'), parts along dimension 1
- grad_down: bfloat16 [16, 8192, 1024], P('tile', 'groups'), parts along dimension 1
The draws below stay inside these ranges and needn't reach their ends.
There are 2 independent parts, one for each index of `groups`. The reference program is written for one: setup_inputs(seed, part) draws one part's arguments, and reference() takes and returns one part's arrays. A program takes and returns all parts, laid end to end along the dimension named above; an argument that names none is the same for every part. Nothing has to cross between parts.
All inputs are finite; a program needn't handle non-finite values.
Results may differ from the reference program's by a relative error of at most 0.0062.
Values may be sent and summed in bfloat16 or wider, within the bound.
No kernel may reach another device: no remote copies, remote signals or barrier semaphores. Data moves between devices by JAX's collectives and lax.ppermute only.
A program may use at most 256 MiB of HBM per device.

```python
import jax
import jax.numpy as jnp
from jax import lax

D = 4096
FF = 16384
Q = 4
TOKENS = 1024
CELLS = 16
GROUP = 4


def level_of(rng, extent, shards, smallest, top_value):
    def one(position, shards_of):
        draws = jax.random.uniform(jax.random.fold_in(jax.random.fold_in(rng, 6), position), (shards_of,), jnp.float32, smallest / len(shards), top_value / len(shards))
        return jnp.repeat(jnp.exp(draws), extent[position] // shards_of).reshape((-1,) + (1,) * (len(extent) - position - 1))

    gain = one(*shards[0])
    for cut in shards[1:]:
        gain = gain * one(*cut)
    return gain


def bell_draw(key, shape, scale, bound, split=(), dtype=jnp.bfloat16):
    array = scale * jax.random.normal(key, shape, jnp.float32)
    if split:
        array = array * level_of(key, shape, split, -0.22, 0.18)
    return jnp.clip(array, -bound, bound).astype(dtype)


def setup_inputs(seed: int = 0, part: int = 0) -> dict:
    seeds = jax.random.split(jax.random.key(seed), 5)
    own_keys = jax.random.split(jax.random.fold_in(seeds[4], part), 5)
    hidden_in = bell_draw(own_keys[0], (TOKENS, D), 1.0, 6.0, ((1, 16),))
    w_up = bell_draw(seeds[1], (CELLS, D // Q, FF // GROUP), D ** -0.5, 0.09375, ((0, 16),))
    w_down = bell_draw(seeds[2], (CELLS, FF // GROUP, D // Q), FF ** -0.5, 0.046875, ((0, 16),))
    out_grad = bell_draw(own_keys[3], (TOKENS, D), 1.0, 6.0, ((1, 16),))
    return {"hidden_in": hidden_in, "w_up": w_up, "w_down": w_down, "out_grad": out_grad}


root_half = 0.7071067811865476
inv_root_tau = 0.3989422804014327


def gelu_value(values):
    return 0.5 * values * (1.0 + lax.erf(values * root_half))


def gelu_slope(values):
    return 0.5 * (1.0 + lax.erf(values * root_half)) + values * jnp.exp(-0.5 * values * values) * inv_root_tau


def reference(hidden_in, w_up, w_down, out_grad):
    up_full = w_up.reshape(Q, GROUP, D // Q, FF // GROUP).transpose(0, 2, 1, 3).reshape(D, FF)
    down_full = w_down.reshape(Q, GROUP, FF // GROUP, D // Q).transpose(1, 2, 0, 3).reshape(FF, D)
    width_block = D // Q
    preact = jnp.zeros((TOKENS, FF), jnp.float32)
    act_grad = jnp.zeros((TOKENS, FF), jnp.float32)
    for column_block in range(Q):
        start_col = column_block * width_block
        stop_col = start_col + width_block
        partial_value = jnp.dot(hidden_in[:, start_col:stop_col], up_full[start_col:stop_col], preferred_element_type=jnp.float32)
        preact = preact + lax.optimization_barrier(partial_value.astype(jnp.bfloat16)).astype(jnp.float32)
        partial_grad = jnp.dot(out_grad[:, start_col:stop_col], down_full[:, start_col:stop_col].T, preferred_element_type=jnp.float32)
        act_grad = act_grad + lax.optimization_barrier(partial_grad.astype(jnp.bfloat16)).astype(jnp.float32)
    activation = gelu_value(preact).astype(jnp.bfloat16)
    block_out = (hidden_in.astype(jnp.float32) + jnp.dot(activation, down_full, preferred_element_type=jnp.float32)).astype(jnp.bfloat16)
    pre_grad = (act_grad * gelu_slope(preact)).astype(jnp.bfloat16)
    grad_down_full = jnp.dot(activation.T, out_grad, preferred_element_type=jnp.float32).astype(jnp.bfloat16)
    grad_up_full = jnp.dot(hidden_in.T, pre_grad, preferred_element_type=jnp.float32).astype(jnp.bfloat16)
    input_grad = (out_grad.astype(jnp.float32) + jnp.dot(pre_grad, up_full.T, preferred_element_type=jnp.float32)).astype(jnp.bfloat16)
    grad_up = grad_up_full.reshape(Q, D // Q, GROUP, FF // GROUP).transpose(0, 2, 1, 3).reshape(CELLS, D // Q, FF // GROUP)
    grad_down = grad_down_full.reshape(GROUP, FF // GROUP, Q, D // Q).transpose(2, 0, 1, 3).reshape(CELLS, FF // GROUP, D // Q)
    return block_out, input_grad, grad_up, grad_down
```

```python
import jax
import jax.numpy as jnp
import numpy as np
from jax import lax
from jax.sharding import Mesh
from jax.sharding import PartitionSpec as P


root_half = 0.7071067811865476
inv_root_tau = 0.3989422804014327


def gelu_value(values):
    return 0.5 * values * (1.0 + lax.erf(values * root_half))


def gelu_slope(values):
    return (
        0.5 * (1.0 + lax.erf(values * root_half))
        + values * jnp.exp(-0.5 * values * values) * inv_root_tau
    )


def cycle_reduce(terms):
    count = lax.axis_size("r")
    pos = lax.axis_index("r")
    block_rows = terms.shape[0] // count
    shares = terms.reshape(count, block_rows, terms.shape[1])
    summed = lax.dynamic_index_in_dim(shares, pos, 0, keepdims=False).astype(jnp.float32)
    for distance in range(1, count):
        outgoing = lax.dynamic_index_in_dim(shares, (pos + distance) % count, 0, keepdims=False)
        incoming = lax.ppermute(
            outgoing, "r", [(i, (i + distance) % count) for i in range(count)]
        )
        summed = summed + incoming.astype(jnp.float32)
    return summed


def on_device(hidden_in, w_up, w_down, out_grad):
    up_tile = w_up[0]
    down_tile = w_down[0]
    x_rows = lax.all_gather(hidden_in, "p", axis=1, tiled=True)
    up_terms = jnp.dot(x_rows, up_tile, preferred_element_type=jnp.float32).astype(jnp.bfloat16)
    preact = cycle_reduce(up_terms)
    activation = lax.all_gather(gelu_value(preact).astype(jnp.bfloat16), "r", axis=0, tiled=True)
    out_part = jnp.dot(activation, down_tile, preferred_element_type=jnp.float32)
    block_out = (
        hidden_in.astype(jnp.float32)
        + lax.psum_scatter(out_part, "p", scatter_dimension=1, tiled=True)
    ).astype(jnp.bfloat16)

    grad_rows = lax.all_gather(out_grad, "p", axis=1, tiled=True)
    grad_terms = lax.dot_general(
        grad_rows, down_tile, (((1,), (1,)), ((), ())), preferred_element_type=jnp.float32
    ).astype(jnp.bfloat16)
    act_grad = cycle_reduce(grad_terms)
    pre_grad = lax.all_gather(
        (act_grad * gelu_slope(preact)).astype(jnp.bfloat16), "r", axis=0, tiled=True
    )
    grad_down = lax.dot_general(
        activation, grad_rows, (((0,), (0,)), ((), ())), preferred_element_type=jnp.float32
    ).astype(jnp.bfloat16)
    grad_up = lax.dot_general(
        x_rows, pre_grad, (((0,), (0,)), ((), ())), preferred_element_type=jnp.float32
    ).astype(jnp.bfloat16)
    back_part = lax.dot_general(
        pre_grad, up_tile, (((1,), (1,)), ((), ())), preferred_element_type=jnp.float32
    )
    input_grad = (
        out_grad.astype(jnp.float32)
        + lax.psum_scatter(back_part, "p", scatter_dimension=1, tiled=True)
    ).astype(jnp.bfloat16)
    return (block_out, input_grad, grad_up[None], grad_down[None])


def solution(mesh):
    groups = mesh.shape["groups"]
    tile = mesh.shape["tile"]

    def run(hidden_in, w_up, w_down, out_grad):
        width_blocks = hidden_in.shape[1] // w_up.shape[1]
        grid = Mesh(
            np.asarray(mesh.devices).reshape(groups, width_blocks, tile // width_blocks),
            ("groups", "r", "p"),
        )
        cells = ("r", "p")
        return jax.shard_map(
            on_device,
            mesh=grid,
            in_specs=(
                P("groups", cells),
                P(cells, None, None),
                P(cells, None, None),
                P("groups", cells),
            ),
            out_specs=(
                P("groups", cells),
                P("groups", cells),
                P(cells, "groups", None),
                P(cells, "groups", None),
            ),
            check_vma=False,
        )(hidden_in, w_up, w_down, out_grad)

    return run
```

```python
import jax
import jax.numpy as jnp
import numpy as np
from jax import lax
from jax.sharding import Mesh
from jax.sharding import PartitionSpec as P


root_half = 0.7071067811865476
inv_root_tau = 0.3989422804014327


def gelu_value(values):
    return 0.5 * values * (1.0 + lax.erf(values * root_half))


def gelu_slope(values):
    return (
        0.5 * (1.0 + lax.erf(values * root_half))
        + values * jnp.exp(-0.5 * values * values) * inv_root_tau
    )


def line_reduce(terms):
    count = lax.axis_size("r")
    pos = lax.axis_index("r")
    block_rows = terms.shape[0] // count
    shares = terms.reshape(count, block_rows, terms.shape[1])
    up_in = jnp.zeros((block_rows, terms.shape[1]), jnp.float32)
    down_in = jnp.zeros((block_rows, terms.shape[1]), jnp.float32)
    for step in range(count - 1):
        up_block = jnp.clip(count - 1 - step + pos, 0, count - 1)
        up_out = (up_in + lax.dynamic_index_in_dim(shares, up_block, 0, keepdims=False)).astype(
            jnp.bfloat16
        )
        down_block = jnp.clip(pos + step - (count - 1), 0, count - 1)
        down_out = (
            down_in + lax.dynamic_index_in_dim(shares, down_block, 0, keepdims=False)
        ).astype(jnp.bfloat16)
        up_in = lax.ppermute(
            up_out, "r", [(i, i + 1) for i in range(0, step + 1)]
        ).astype(jnp.float32)
        down_in = lax.ppermute(
            down_out, "r", [(i, i - 1) for i in range(count - 1 - step, count)]
        ).astype(jnp.float32)
    own = lax.dynamic_index_in_dim(shares, pos, 0, keepdims=False).astype(jnp.float32)
    return up_in + own + down_in


def line_gather(block):
    count = lax.axis_size("r")
    pos = lax.axis_index("r")
    ups, downs = [], []
    up_out = down_out = block
    for step in range(count - 1):
        up_out = lax.ppermute(up_out, "r", [(i, i + 1) for i in range(step, count - 1)])
        down_out = lax.ppermute(down_out, "r", [(i, i - 1) for i in range(1, count - step)])
        ups.append(up_out)
        downs.append(down_out)
    cases = [block] + ups + downs
    pieces = []
    for k in range(count):
        which = jnp.where(
            pos == k, 0, jnp.where(pos > k, pos - k, count - 1 + k - pos)
        ).astype(jnp.int32)
        pieces.append(lax.select_n(which, *cases))
    return jnp.concatenate(pieces, axis=0)


def on_device(hidden_in, w_up, w_down, out_grad):
    up_tile = w_up[0]
    down_tile = w_down[0]
    x_rows = lax.all_gather(hidden_in, "p", axis=1, tiled=True)
    up_terms = jnp.dot(x_rows, up_tile, preferred_element_type=jnp.float32).astype(jnp.bfloat16)
    preact = line_reduce(up_terms)
    activation = line_gather(gelu_value(preact).astype(jnp.bfloat16))
    out_part = jnp.dot(activation, down_tile, preferred_element_type=jnp.float32)
    block_out = (
        hidden_in.astype(jnp.float32)
        + lax.psum_scatter(out_part, "p", scatter_dimension=1, tiled=True)
    ).astype(jnp.bfloat16)

    grad_rows = lax.all_gather(out_grad, "p", axis=1, tiled=True)
    grad_terms = lax.dot_general(
        grad_rows, down_tile, (((1,), (1,)), ((), ())), preferred_element_type=jnp.float32
    ).astype(jnp.bfloat16)
    act_grad = line_reduce(grad_terms)
    pre_grad = line_gather((act_grad * gelu_slope(preact)).astype(jnp.bfloat16))
    grad_down = lax.dot_general(
        activation, grad_rows, (((0,), (0,)), ((), ())), preferred_element_type=jnp.float32
    ).astype(jnp.bfloat16)
    grad_up = lax.dot_general(
        x_rows, pre_grad, (((0,), (0,)), ((), ())), preferred_element_type=jnp.float32
    ).astype(jnp.bfloat16)
    back_part = lax.dot_general(
        pre_grad, up_tile, (((1,), (1,)), ((), ())), preferred_element_type=jnp.float32
    )
    input_grad = (
        out_grad.astype(jnp.float32)
        + lax.psum_scatter(back_part, "p", scatter_dimension=1, tiled=True)
    ).astype(jnp.bfloat16)
    return (block_out, input_grad, grad_up[None], grad_down[None])


def solution(mesh):
    groups = mesh.shape["groups"]
    tile = mesh.shape["tile"]

    def run(hidden_in, w_up, w_down, out_grad):
        width_blocks = hidden_in.shape[1] // w_up.shape[1]
        grid = Mesh(
            np.asarray(mesh.devices).reshape(groups, width_blocks, tile // width_blocks),
            ("groups", "r", "p"),
        )
        cells = ("r", "p")
        return jax.shard_map(
            on_device,
            mesh=grid,
            in_specs=(
                P("groups", cells),
                P(cells, None, None),
                P(cells, None, None),
                P("groups", cells),
            ),
            out_specs=(
                P("groups", cells),
                P("groups", cells),
                P(cells, "groups", None),
                P(cells, "groups", None),
            ),
            check_vma=False,
        )(hidden_in, w_up, w_down, out_grad)

    return run
```

```python
import jax
import jax.numpy as jnp
import numpy as np
from jax import lax
from jax.sharding import Mesh
from jax.sharding import PartitionSpec as P


root_half = 0.7071067811865476
inv_root_tau = 0.3989422804014327


def gelu_value(values):
    return 0.5 * values * (1.0 + lax.erf(values * root_half))


def gelu_slope(values):
    return (
        0.5 * (1.0 + lax.erf(values * root_half))
        + values * jnp.exp(-0.5 * values * values) * inv_root_tau
    )


class LineReduce:
    def __init__(self, terms):
        self.count = lax.axis_size("r")
        self.pos = lax.axis_index("r")
        rows = terms.shape[0] // self.count
        self.shares = terms.reshape(self.count, rows, terms.shape[1])
        self.up_in = jnp.zeros((rows, terms.shape[1]), jnp.float32)
        self.down_in = jnp.zeros((rows, terms.shape[1]), jnp.float32)

    def senders(self, step):
        return (0, step), (self.count - 1 - step, self.count - 1)

    def payload(self, step):
        last = self.count - 1
        up_block = jnp.clip(last - step + self.pos, 0, last)
        down_block = jnp.clip(self.pos + step - last, 0, last)
        up = self.up_in + lax.dynamic_index_in_dim(self.shares, up_block, 0, keepdims=False)
        down = self.down_in + lax.dynamic_index_in_dim(self.shares, down_block, 0, keepdims=False)
        return up.astype(jnp.bfloat16), down.astype(jnp.bfloat16)

    def receive(self, step, up, down):
        self.up_in = up.astype(jnp.float32)
        self.down_in = down.astype(jnp.float32)

    def result(self):
        own = lax.dynamic_index_in_dim(self.shares, self.pos, 0, keepdims=False)
        return self.up_in + own.astype(jnp.float32) + self.down_in


class LineGather:
    def __init__(self, block):
        self.count = lax.axis_size("r")
        self.pos = lax.axis_index("r")
        self.block = block
        self.up_cur = self.down_cur = block
        self.ups, self.downs = [], []

    def senders(self, step):
        return (step, self.count - 2), (1, self.count - 1 - step)

    def payload(self, step):
        return self.up_cur, self.down_cur

    def receive(self, step, up, down):
        self.up_cur, self.down_cur = up, down
        self.ups.append(up)
        self.downs.append(down)

    def result(self):
        count, pos = self.count, self.pos
        cases = [self.block] + self.ups + self.downs
        pieces = []
        for k in range(count):
            which = jnp.where(pos == k, 0, jnp.where(pos > k, pos - k, count - 1 + k - pos))
            pieces.append(lax.select_n(which.astype(jnp.int32), *cases))
        return jnp.concatenate(pieces, axis=0)


def run_slot(entries):
    pos = lax.axis_index("r")
    loads = [entry.payload(step) for entry, step in entries]
    ranges = [entry.senders(step) for entry, step in entries]
    received = []
    for direction, shift in ((0, 1), (1, -1)):
        combined = None
        pairs = []
        for load, rng in zip(loads, ranges):
            lo, hi = rng[direction]
            if lo > hi:
                continue
            pairs += [(i, i + shift) for i in range(lo, hi + 1)]
            mine = (pos >= lo) & (pos <= hi)
            combined = load[direction] if combined is None else jnp.where(mine, load[direction], combined)
        if combined is None:
            received.append(None)
            continue
        received.append(lax.ppermute(combined, "r", pairs))
    for (entry, step), load, rng in zip(entries, loads, ranges):
        parts = []
        for direction, shift in ((0, 1), (1, -1)):
            lo, hi = rng[direction]
            got = received[direction]
            if got is None or lo > hi:
                parts.append(jnp.zeros_like(load[direction]))
                continue
            mine = (pos >= lo + shift) & (pos <= hi + shift)
            parts.append(jnp.where(mine, got, jnp.zeros_like(got)))
        entry.receive(step, *parts)


def on_device(hidden_in, w_up, w_down, out_grad):
    up_tile = w_up[0]
    down_tile = w_down[0]
    count = lax.axis_size("r")
    x_rows = lax.all_gather(hidden_in, "p", axis=1, tiled=True)
    up_terms = jnp.dot(x_rows, up_tile, preferred_element_type=jnp.float32).astype(jnp.bfloat16)
    grad_rows = lax.all_gather(out_grad, "p", axis=1, tiled=True)
    grad_terms = lax.dot_general(
        grad_rows, down_tile, (((1,), (1,)), ((), ())), preferred_element_type=jnp.float32
    ).astype(jnp.bfloat16)

    up_sum = LineReduce(up_terms)
    grad_sum = LineReduce(grad_terms)
    for step in range(count - 1):
        run_slot([(up_sum, step)])
    preact = up_sum.result()
    act_gather = LineGather(gelu_value(preact).astype(jnp.bfloat16))
    if count > 1:
        run_slot([(act_gather, 0)])
    for step in range(1, count - 1):
        run_slot([(act_gather, step), (grad_sum, step - 1)])
    if count > 1:
        run_slot([(grad_sum, count - 2)])
    act_grad = grad_sum.result()
    pre_gather = LineGather((act_grad * gelu_slope(preact)).astype(jnp.bfloat16))
    for step in range(count - 1):
        run_slot([(pre_gather, step)])
    activation = act_gather.result()
    pre_grad = pre_gather.result()

    out_part = jnp.dot(activation, down_tile, preferred_element_type=jnp.float32)
    block_out = (
        hidden_in.astype(jnp.float32)
        + lax.psum_scatter(out_part, "p", scatter_dimension=1, tiled=True)
    ).astype(jnp.bfloat16)
    grad_down = lax.dot_general(
        activation, grad_rows, (((0,), (0,)), ((), ())), preferred_element_type=jnp.float32
    ).astype(jnp.bfloat16)
    grad_up = lax.dot_general(
        x_rows, pre_grad, (((0,), (0,)), ((), ())), preferred_element_type=jnp.float32
    ).astype(jnp.bfloat16)
    back_part = lax.dot_general(
        pre_grad, up_tile, (((1,), (1,)), ((), ())), preferred_element_type=jnp.float32
    )
    input_grad = (
        out_grad.astype(jnp.float32)
        + lax.psum_scatter(back_part, "p", scatter_dimension=1, tiled=True)
    ).astype(jnp.bfloat16)
    return (block_out, input_grad, grad_up[None], grad_down[None])


def solution(mesh):
    groups = mesh.shape["groups"]
    tile = mesh.shape["tile"]

    def run(hidden_in, w_up, w_down, out_grad):
        width_blocks = hidden_in.shape[1] // w_up.shape[1]
        grid = Mesh(
            np.asarray(mesh.devices).reshape(groups, width_blocks, tile // width_blocks),
            ("groups", "r", "p"),
        )
        cells = ("r", "p")
        return jax.shard_map(
            on_device,
            mesh=grid,
            in_specs=(
                P("groups", cells),
                P(cells, None, None),
                P(cells, None, None),
                P("groups", cells),
            ),
            out_specs=(
                P("groups", cells),
                P("groups", cells),
                P(cells, "groups", None),
                P(cells, "groups", None),
            ),
            check_vma=False,
        )(hidden_in, w_up, w_down, out_grad)

    return run
```

```python
import jax
import jax.numpy as jnp
import numpy as np
from jax import lax
from jax.sharding import Mesh
from jax.sharding import PartitionSpec as P


root_half = 0.7071067811865476
inv_root_tau = 0.3989422804014327


def gelu_value(values):
    return 0.5 * values * (1.0 + lax.erf(values * root_half))


def gelu_slope(values):
    return (
        0.5 * (1.0 + lax.erf(values * root_half))
        + values * jnp.exp(-0.5 * values * values) * inv_root_tau
    )


class LineReduce:
    def __init__(self, terms):
        self.count = lax.axis_size("r")
        self.pos = lax.axis_index("r")
        rows = terms.shape[0] // self.count
        self.shares = terms.reshape(self.count, rows, terms.shape[1])
        self.up_in = jnp.zeros((rows, terms.shape[1]), jnp.float32)
        self.down_in = jnp.zeros((rows, terms.shape[1]), jnp.float32)

    def senders(self, step):
        return (0, step), (self.count - 1 - step, self.count - 1)

    def payload(self, step):
        last = self.count - 1
        up_block = jnp.clip(last - step + self.pos, 0, last)
        down_block = jnp.clip(self.pos + step - last, 0, last)
        up = self.up_in + lax.dynamic_index_in_dim(self.shares, up_block, 0, keepdims=False)
        down = self.down_in + lax.dynamic_index_in_dim(self.shares, down_block, 0, keepdims=False)
        return up.astype(jnp.bfloat16), down.astype(jnp.bfloat16)

    def receive(self, step, up, down):
        self.up_in = up.astype(jnp.float32)
        self.down_in = down.astype(jnp.float32)

    def result(self):
        own = lax.dynamic_index_in_dim(self.shares, self.pos, 0, keepdims=False)
        return self.up_in + own.astype(jnp.float32) + self.down_in


class LineGather:
    def __init__(self, block):
        self.count = lax.axis_size("r")
        self.pos = lax.axis_index("r")
        self.block = block
        self.up_cur = self.down_cur = block
        self.ups, self.downs = [], []

    def senders(self, step):
        return (step, self.count - 2), (1, self.count - 1 - step)

    def payload(self, step):
        return self.up_cur, self.down_cur

    def receive(self, step, up, down):
        self.up_cur, self.down_cur = up, down
        self.ups.append(up)
        self.downs.append(down)

    def result(self):
        count, pos = self.count, self.pos
        cases = [self.block] + self.ups + self.downs
        pieces = []
        for k in range(count):
            which = jnp.where(pos == k, 0, jnp.where(pos > k, pos - k, count - 1 + k - pos))
            pieces.append(lax.select_n(which.astype(jnp.int32), *cases))
        return jnp.concatenate(pieces, axis=0)


def run_slot(entries):
    pos = lax.axis_index("r")
    loads = [entry.payload(step) for entry, step in entries]
    ranges = [entry.senders(step) for entry, step in entries]
    received = []
    for direction, shift in ((0, 1), (1, -1)):
        combined = None
        pairs = []
        for load, rng in zip(loads, ranges):
            lo, hi = rng[direction]
            if lo > hi:
                continue
            pairs += [(i, i + shift) for i in range(lo, hi + 1)]
            mine = (pos >= lo) & (pos <= hi)
            combined = load[direction] if combined is None else jnp.where(mine, load[direction], combined)
        if combined is None:
            received.append(None)
            continue
        received.append(lax.ppermute(combined, "r", pairs))
    for (entry, step), load, rng in zip(entries, loads, ranges):
        parts = []
        for direction, shift in ((0, 1), (1, -1)):
            lo, hi = rng[direction]
            got = received[direction]
            if got is None or lo > hi:
                parts.append(jnp.zeros_like(load[direction]))
                continue
            mine = (pos >= lo + shift) & (pos <= hi + shift)
            parts.append(jnp.where(mine, got, jnp.zeros_like(got)))
        entry.receive(step, *parts)


def on_device(hidden_in, w_up, w_down, out_grad):
    up_tile = w_up[0]
    down_tile = w_down[0]
    count = lax.axis_size("r")
    x_rows = lax.all_gather(hidden_in, "p", axis=1, tiled=True)
    up_terms = jnp.dot(x_rows, up_tile, preferred_element_type=jnp.float32).astype(jnp.bfloat16)
    grad_rows = lax.all_gather(out_grad, "p", axis=1, tiled=True)
    grad_terms = lax.dot_general(
        grad_rows, down_tile, (((1,), (1,)), ((), ())), preferred_element_type=jnp.float32
    ).astype(jnp.bfloat16)

    up_sum = LineReduce(up_terms)
    if count > 1:
        run_slot([(up_sum, 0)])
        up_sum.up_in, up_sum.down_in, grad_terms = lax.optimization_barrier(
            (up_sum.up_in, up_sum.down_in, grad_terms)
        )
    grad_sum = LineReduce(grad_terms)
    for step in range(1, count - 1):
        run_slot([(up_sum, step)])
    preact = up_sum.result()
    act_gather = LineGather(gelu_value(preact).astype(jnp.bfloat16))
    if count > 1:
        run_slot([(act_gather, 0)])
    for step in range(1, count - 1):
        run_slot([(act_gather, step), (grad_sum, step - 1)])
    activation = act_gather.result()
    out_part = jnp.dot(activation, down_tile, preferred_element_type=jnp.float32)
    out_sum = lax.psum_scatter(out_part, "p", scatter_dimension=1, tiled=True)
    grad_down = lax.dot_general(
        activation, grad_rows, (((0,), (0,)), ((), ())), preferred_element_type=jnp.float32
    ).astype(jnp.bfloat16)
    if count > 1:
        run_slot([(grad_sum, count - 2)])
    act_grad = grad_sum.result()
    pre_gather = LineGather((act_grad * gelu_slope(preact)).astype(jnp.bfloat16))
    for step in range(count - 1):
        run_slot([(pre_gather, step)])
        if step == min(1, count - 2):
            pre_gather.up_cur, pre_gather.down_cur, out_sum, grad_down = lax.optimization_barrier(
                (pre_gather.up_cur, pre_gather.down_cur, out_sum, grad_down)
            )
            pre_gather.ups[-1], pre_gather.downs[-1] = pre_gather.up_cur, pre_gather.down_cur
    pre_grad = pre_gather.result()
    block_out = (hidden_in.astype(jnp.float32) + out_sum).astype(jnp.bfloat16)
    grad_up = lax.dot_general(
        x_rows, pre_grad, (((0,), (0,)), ((), ())), preferred_element_type=jnp.float32
    ).astype(jnp.bfloat16)
    back_part = lax.dot_general(
        pre_grad, up_tile, (((1,), (1,)), ((), ())), preferred_element_type=jnp.float32
    )
    input_grad = (
        out_grad.astype(jnp.float32)
        + lax.psum_scatter(back_part, "p", scatter_dimension=1, tiled=True)
    ).astype(jnp.bfloat16)
    return (block_out, input_grad, grad_up[None], grad_down[None])


def solution(mesh):
    groups = mesh.shape["groups"]
    tile = mesh.shape["tile"]

    def run(hidden_in, w_up, w_down, out_grad):
        width_blocks = hidden_in.shape[1] // w_up.shape[1]
        grid = Mesh(
            np.asarray(mesh.devices).reshape(groups, width_blocks, tile // width_blocks),
            ("groups", "r", "p"),
        )
        cells = ("r", "p")
        return jax.shard_map(
            on_device,
            mesh=grid,
            in_specs=(
                P("groups", cells),
                P(cells, None, None),
                P(cells, None, None),
                P("groups", cells),
            ),
            out_specs=(
                P("groups", cells),
                P("groups", cells),
                P(cells, "groups", None),
                P(cells, "groups", None),
            ),
            check_vma=False,
        )(hidden_in, w_up, w_down, out_grad)

    return run
```

```python
import jax
import jax.numpy as jnp
import numpy as np
from jax import lax
from jax.sharding import Mesh
from jax.sharding import PartitionSpec as P


root_half = 0.7071067811865476
inv_root_tau = 0.3989422804014327


def gelu_value(values):
    return 0.5 * values * (1.0 + lax.erf(values * root_half))


def gelu_slope(values):
    return (
        0.5 * (1.0 + lax.erf(values * root_half))
        + values * jnp.exp(-0.5 * values * values) * inv_root_tau
    )


class LineReduce:
    def __init__(self, terms):
        self.count = lax.axis_size("r")
        self.pos = lax.axis_index("r")
        rows = terms.shape[0] // self.count
        self.shares = terms.reshape(self.count, rows, terms.shape[1])
        self.up_in = jnp.zeros((rows, terms.shape[1]), jnp.float32)
        self.down_in = jnp.zeros((rows, terms.shape[1]), jnp.float32)

    def senders(self, step):
        return (0, step), (self.count - 1 - step, self.count - 1)

    def payload(self, step):
        last = self.count - 1
        up_block = jnp.clip(last - step + self.pos, 0, last)
        down_block = jnp.clip(self.pos + step - last, 0, last)
        up = self.up_in + lax.dynamic_index_in_dim(self.shares, up_block, 0, keepdims=False)
        down = self.down_in + lax.dynamic_index_in_dim(self.shares, down_block, 0, keepdims=False)
        return up.astype(jnp.bfloat16), down.astype(jnp.bfloat16)

    def receive(self, step, up, down):
        self.up_in = up.astype(jnp.float32)
        self.down_in = down.astype(jnp.float32)

    def result(self):
        own = lax.dynamic_index_in_dim(self.shares, self.pos, 0, keepdims=False)
        return self.up_in + own.astype(jnp.float32) + self.down_in


class LineGather:
    def __init__(self, block):
        self.count = lax.axis_size("r")
        self.pos = lax.axis_index("r")
        self.block = block
        self.up_cur = self.down_cur = block
        self.ups, self.downs = [], []

    def senders(self, step):
        return (step, self.count - 2), (1, self.count - 1 - step)

    def payload(self, step):
        return self.up_cur, self.down_cur

    def receive(self, step, up, down):
        self.up_cur, self.down_cur = up, down
        self.ups.append(up)
        self.downs.append(down)

    def result(self):
        count, pos = self.count, self.pos
        cases = [self.block] + self.ups + self.downs
        pieces = []
        for k in range(count):
            which = jnp.where(pos == k, 0, jnp.where(pos > k, pos - k, count - 1 + k - pos))
            pieces.append(lax.select_n(which.astype(jnp.int32), *cases))
        return jnp.concatenate(pieces, axis=0)


def run_slot(entries):
    pos = lax.axis_index("r")
    loads = [entry.payload(step) for entry, step in entries]
    ranges = [entry.senders(step) for entry, step in entries]
    received = []
    for direction, shift in ((0, 1), (1, -1)):
        combined = None
        pairs = []
        for load, rng in zip(loads, ranges):
            lo, hi = rng[direction]
            if lo > hi:
                continue
            pairs += [(i, i + shift) for i in range(lo, hi + 1)]
            mine = (pos >= lo) & (pos <= hi)
            combined = load[direction] if combined is None else jnp.where(mine, load[direction], combined)
        if combined is None:
            received.append(None)
            continue
        received.append(lax.ppermute(combined, "r", pairs))
    for (entry, step), load, rng in zip(entries, loads, ranges):
        parts = []
        for direction, shift in ((0, 1), (1, -1)):
            lo, hi = rng[direction]
            got = received[direction]
            if got is None or lo > hi:
                parts.append(jnp.zeros_like(load[direction]))
                continue
            mine = (pos >= lo + shift) & (pos <= hi + shift)
            parts.append(jnp.where(mine, got, jnp.zeros_like(got)))
        entry.receive(step, *parts)


def on_device(hidden_in, w_up, w_down, out_grad):
    up_tile = w_up[0]
    down_tile = w_down[0]
    count = lax.axis_size("r")
    x_rows = lax.all_gather(hidden_in, "p", axis=1, tiled=True)
    up_terms = jnp.dot(x_rows, up_tile, preferred_element_type=jnp.float32).astype(jnp.bfloat16)
    grad_rows = lax.all_gather(out_grad, "p", axis=1, tiled=True)
    grad_terms = lax.dot_general(
        grad_rows, down_tile, (((1,), (1,)), ((), ())), preferred_element_type=jnp.float32
    ).astype(jnp.bfloat16)

    up_sum = LineReduce(up_terms)
    if count > 1:
        run_slot([(up_sum, 0)])
        up_sum.up_in, up_sum.down_in, grad_terms = lax.optimization_barrier(
            (up_sum.up_in, up_sum.down_in, grad_terms)
        )
    grad_sum = LineReduce(grad_terms)
    for step in range(1, count - 1):
        run_slot([(up_sum, step)])
    preact = up_sum.result()
    act_gather = LineGather(gelu_value(preact).astype(jnp.bfloat16))
    if count > 1:
        run_slot([(act_gather, 0)])
    for step in range(1, count - 1):
        run_slot([(act_gather, step), (grad_sum, step - 1)])
    activation = act_gather.result()
    out_part = jnp.dot(activation, down_tile, preferred_element_type=jnp.float32)
    grad_down = lax.dot_general(
        activation, grad_rows, (((0,), (0,)), ((), ())), preferred_element_type=jnp.float32
    ).astype(jnp.bfloat16)
    if count > 1:
        run_slot([(grad_sum, count - 2)])
        grad_sum.up_in, grad_sum.down_in, out_part = lax.optimization_barrier(
            (grad_sum.up_in, grad_sum.down_in, out_part)
        )
    out_sum = lax.psum_scatter(out_part, "p", scatter_dimension=1, tiled=True)
    act_grad = grad_sum.result()
    pre_gather = LineGather((act_grad * gelu_slope(preact)).astype(jnp.bfloat16))
    tied = {0: "grad_down", min(1, count - 2): "out_sum"}
    for step in range(count - 1):
        run_slot([(pre_gather, step)])
        for name in [tied.get(0), tied.get(1)] if step == 0 and count == 2 else [tied.get(step)]:
            if name is None:
                continue
            value = grad_down if name == "grad_down" else out_sum
            pre_gather.up_cur, pre_gather.down_cur, value = lax.optimization_barrier(
                (pre_gather.up_cur, pre_gather.down_cur, value)
            )
            pre_gather.ups[-1], pre_gather.downs[-1] = pre_gather.up_cur, pre_gather.down_cur
            if name == "grad_down":
                grad_down = value
            else:
                out_sum = value
    pre_grad = pre_gather.result()
    block_out = (hidden_in.astype(jnp.float32) + out_sum).astype(jnp.bfloat16)
    grad_up = lax.dot_general(
        x_rows, pre_grad, (((0,), (0,)), ((), ())), preferred_element_type=jnp.float32
    ).astype(jnp.bfloat16)
    back_part = lax.dot_general(
        pre_grad, up_tile, (((1,), (1,)), ((), ())), preferred_element_type=jnp.float32
    )
    input_grad = (
        out_grad.astype(jnp.float32)
        + lax.psum_scatter(back_part, "p", scatter_dimension=1, tiled=True)
    ).astype(jnp.bfloat16)
    return (block_out, input_grad, grad_up[None], grad_down[None])


def solution(mesh):
    groups = mesh.shape["groups"]
    tile = mesh.shape["tile"]

    def run(hidden_in, w_up, w_down, out_grad):
        width_blocks = hidden_in.shape[1] // w_up.shape[1]
        grid = Mesh(
            np.asarray(mesh.devices).reshape(groups, width_blocks, tile // width_blocks),
            ("groups", "r", "p"),
        )
        cells = ("r", "p")
        return jax.shard_map(
            on_device,
            mesh=grid,
            in_specs=(
                P("groups", cells),
                P(cells, None, None),
                P(cells, None, None),
                P("groups", cells),
            ),
            out_specs=(
                P("groups", cells),
                P("groups", cells),
                P(cells, "groups", None),
                P(cells, "groups", None),
            ),
            check_vma=False,
        )(hidden_in, w_up, w_down, out_grad)

    return run
```

```python
import jax
import jax.numpy as jnp
import numpy as np
from jax import lax
from jax.sharding import Mesh
from jax.sharding import PartitionSpec as P


root_half = 0.7071067811865476
inv_root_tau = 0.3989422804014327


def gelu_value(values):
    return 0.5 * values * (1.0 + lax.erf(values * root_half))


def gelu_slope(values):
    return (
        0.5 * (1.0 + lax.erf(values * root_half))
        + values * jnp.exp(-0.5 * values * values) * inv_root_tau
    )


class LineReduce:
    def __init__(self, terms):
        self.count = lax.axis_size("r")
        self.pos = lax.axis_index("r")
        rows = terms.shape[0] // self.count
        self.shares = terms.reshape(self.count, rows, terms.shape[1])
        self.up_in = jnp.zeros((rows, terms.shape[1]), jnp.float32)
        self.down_in = jnp.zeros((rows, terms.shape[1]), jnp.float32)

    def senders(self, step):
        return (0, step), (self.count - 1 - step, self.count - 1)

    def payload(self, step):
        last = self.count - 1
        up_block = jnp.clip(last - step + self.pos, 0, last)
        down_block = jnp.clip(self.pos + step - last, 0, last)
        up = self.up_in + lax.dynamic_index_in_dim(self.shares, up_block, 0, keepdims=False)
        down = self.down_in + lax.dynamic_index_in_dim(self.shares, down_block, 0, keepdims=False)
        return up.astype(jnp.bfloat16), down.astype(jnp.bfloat16)

    def receive(self, step, up, down):
        self.up_in = up.astype(jnp.float32)
        self.down_in = down.astype(jnp.float32)

    def result(self):
        own = lax.dynamic_index_in_dim(self.shares, self.pos, 0, keepdims=False)
        return self.up_in + own.astype(jnp.float32) + self.down_in


class LineGather:
    def __init__(self, block):
        self.count = lax.axis_size("r")
        self.pos = lax.axis_index("r")
        self.block = block
        self.up_cur = self.down_cur = block
        self.ups, self.downs = [], []

    def senders(self, step):
        return (step, self.count - 2), (1, self.count - 1 - step)

    def payload(self, step):
        return self.up_cur, self.down_cur

    def receive(self, step, up, down):
        self.up_cur, self.down_cur = up, down
        self.ups.append(up)
        self.downs.append(down)

    def result(self):
        count, pos = self.count, self.pos
        cases = [self.block] + self.ups + self.downs
        pieces = []
        for k in range(count):
            which = jnp.where(pos == k, 0, jnp.where(pos > k, pos - k, count - 1 + k - pos))
            pieces.append(lax.select_n(which.astype(jnp.int32), *cases))
        return jnp.concatenate(pieces, axis=0)


def run_slot(entries):
    pos = lax.axis_index("r")
    loads = [entry.payload(step) for entry, step in entries]
    ranges = [entry.senders(step) for entry, step in entries]
    received = []
    for direction, shift in ((0, 1), (1, -1)):
        combined = None
        pairs = []
        for load, rng in zip(loads, ranges):
            lo, hi = rng[direction]
            if lo > hi:
                continue
            pairs += [(i, i + shift) for i in range(lo, hi + 1)]
            mine = (pos >= lo) & (pos <= hi)
            combined = load[direction] if combined is None else jnp.where(mine, load[direction], combined)
        if combined is None:
            received.append(None)
            continue
        received.append(lax.ppermute(combined, "r", pairs))
    for (entry, step), load, rng in zip(entries, loads, ranges):
        parts = []
        for direction, shift in ((0, 1), (1, -1)):
            lo, hi = rng[direction]
            got = received[direction]
            if got is None or lo > hi:
                parts.append(jnp.zeros_like(load[direction]))
                continue
            mine = (pos >= lo + shift) & (pos <= hi + shift)
            parts.append(jnp.where(mine, got, jnp.zeros_like(got)))
        entry.receive(step, *parts)


def on_device(hidden_in, w_up, w_down, out_grad):
    up_tile = w_up[0]
    down_tile = w_down[0]
    count = lax.axis_size("r")
    x_rows = lax.all_gather(hidden_in, "p", axis=1, tiled=True)
    up_terms = jnp.dot(x_rows, up_tile, preferred_element_type=jnp.float32).astype(jnp.bfloat16)
    grad_rows = lax.all_gather(out_grad, "p", axis=1, tiled=True)
    grad_terms = lax.dot_general(
        grad_rows, down_tile, (((1,), (1,)), ((), ())), preferred_element_type=jnp.float32
    ).astype(jnp.bfloat16)

    up_sum = LineReduce(up_terms)
    if count > 1:
        run_slot([(up_sum, 0)])
        up_sum.up_in, up_sum.down_in, grad_terms = lax.optimization_barrier(
            (up_sum.up_in, up_sum.down_in, grad_terms)
        )
    grad_sum = LineReduce(grad_terms)
    for step in range(1, count - 1):
        run_slot([(up_sum, step)])
    preact = up_sum.result()
    act_gather = LineGather(gelu_value(preact).astype(jnp.bfloat16))
    if count > 1:
        run_slot([(act_gather, 0)])
    for step in range(1, count - 1):
        run_slot([(act_gather, step), (grad_sum, step - 1)])
    activation = act_gather.result()
    out_part = jnp.dot(activation, down_tile, preferred_element_type=jnp.float32)
    out_sum = lax.psum_scatter(out_part, "p", scatter_dimension=1, tiled=True)
    grad_down = lax.dot_general(
        activation, grad_rows, (((0,), (0,)), ((), ())), preferred_element_type=jnp.float32
    ).astype(jnp.bfloat16)
    if count > 1:
        run_slot([(grad_sum, count - 2)])
    act_grad = grad_sum.result()
    pre_gather = LineGather((act_grad * gelu_slope(preact)).astype(jnp.bfloat16))
    for step in range(count - 1):
        run_slot([(pre_gather, step)])
        if step == min(1, count - 2):
            pre_gather.up_cur, pre_gather.down_cur, out_sum, grad_down = lax.optimization_barrier(
                (pre_gather.up_cur, pre_gather.down_cur, out_sum, grad_down)
            )
            pre_gather.ups[-1], pre_gather.downs[-1] = pre_gather.up_cur, pre_gather.down_cur
    block_out = (hidden_in.astype(jnp.float32) + out_sum).astype(jnp.bfloat16)

    pos = lax.axis_index("r")
    rows = pre_gather.block.shape[0]
    x_blocks = x_rows.reshape(count, rows, x_rows.shape[1])
    pieces = [(pre_gather.block, pos)]
    for step in range(count - 1):
        up_piece, down_piece = pre_gather.ups[step], pre_gather.downs[step]
        up_at, down_at = pos - 1 - step, pos + 1 + step
        if 2 * step + 3 <= count:
            pieces += [(up_piece, up_at), (down_piece, down_at)]
        else:
            pieces.append((up_piece + down_piece, jnp.where(up_at >= 0, up_at, down_at)))
    grad_up = None
    sums = []
    for piece, at in pieces:
        x_block = lax.dynamic_index_in_dim(x_blocks, jnp.clip(at, 0, count - 1), 0, keepdims=False)
        term = lax.dot_general(
            x_block, piece, (((0,), (0,)), ((), ())), preferred_element_type=jnp.float32
        )
        grad_up = term if grad_up is None else grad_up + term
        back_rows = lax.dot_general(
            piece, up_tile, (((1,), (1,)), ((), ())), preferred_element_type=jnp.float32
        )
        sums.append((lax.psum_scatter(back_rows, "p", scatter_dimension=1, tiled=True), at))
    grad_up = grad_up.astype(jnp.bfloat16)
    grad_blocks = out_grad.reshape(count, rows, out_grad.shape[1]).astype(jnp.float32)
    input_rows = []
    for k in range(count):
        total = grad_blocks[k]
        for value, at in sums:
            total = total + jnp.where(at == k, value, jnp.zeros_like(value))
        input_rows.append(total)
    input_grad = jnp.concatenate(input_rows, axis=0).astype(jnp.bfloat16)
    return (block_out, input_grad, grad_up[None], grad_down[None])


def solution(mesh):
    groups = mesh.shape["groups"]
    tile = mesh.shape["tile"]

    def run(hidden_in, w_up, w_down, out_grad):
        width_blocks = hidden_in.shape[1] // w_up.shape[1]
        grid = Mesh(
            np.asarray(mesh.devices).reshape(groups, width_blocks, tile // width_blocks),
            ("groups", "r", "p"),
        )
        cells = ("r", "p")
        return jax.shard_map(
            on_device,
            mesh=grid,
            in_specs=(
                P("groups", cells),
                P(cells, None, None),
                P(cells, None, None),
                P("groups", cells),
            ),
            out_specs=(
                P("groups", cells),
                P("groups", cells),
                P(cells, "groups", None),
                P(cells, "groups", None),
            ),
            check_vma=False,
        )(hidden_in, w_up, w_down, out_grad)

    return run
```

```python
import jax
import jax.numpy as jnp
import numpy as np
from jax import lax
from jax.sharding import Mesh
from jax.sharding import PartitionSpec as P


root_half = 0.7071067811865476
inv_root_tau = 0.3989422804014327


def gelu_value(values):
    return 0.5 * values * (1.0 + lax.erf(values * root_half))


def gelu_slope(values):
    return (
        0.5 * (1.0 + lax.erf(values * root_half))
        + values * jnp.exp(-0.5 * values * values) * inv_root_tau
    )


class LineReduce:
    def __init__(self, terms):
        self.count = lax.axis_size("r")
        self.pos = lax.axis_index("r")
        rows = terms.shape[0] // self.count
        self.shares = terms.reshape(self.count, rows, terms.shape[1])
        self.up_in = jnp.zeros((rows, terms.shape[1]), jnp.float32)
        self.down_in = jnp.zeros((rows, terms.shape[1]), jnp.float32)

    def senders(self, step):
        return (0, step), (self.count - 1 - step, self.count - 1)

    def payload(self, step):
        last = self.count - 1
        up_block = jnp.clip(last - step + self.pos, 0, last)
        down_block = jnp.clip(self.pos + step - last, 0, last)
        up = self.up_in + lax.dynamic_index_in_dim(self.shares, up_block, 0, keepdims=False)
        down = self.down_in + lax.dynamic_index_in_dim(self.shares, down_block, 0, keepdims=False)
        return up.astype(jnp.bfloat16), down.astype(jnp.bfloat16)

    def receive(self, step, up, down):
        self.up_in = up.astype(jnp.float32)
        self.down_in = down.astype(jnp.float32)

    def result(self):
        own = lax.dynamic_index_in_dim(self.shares, self.pos, 0, keepdims=False)
        return self.up_in + own.astype(jnp.float32) + self.down_in


class LineGather:
    def __init__(self, block):
        self.count = lax.axis_size("r")
        self.pos = lax.axis_index("r")
        self.block = block
        self.up_cur = self.down_cur = block
        self.ups, self.downs = [], []

    def senders(self, step):
        return (step, self.count - 2), (1, self.count - 1 - step)

    def payload(self, step):
        return self.up_cur, self.down_cur

    def receive(self, step, up, down):
        self.up_cur, self.down_cur = up, down
        self.ups.append(up)
        self.downs.append(down)

    def result(self):
        count, pos = self.count, self.pos
        cases = [self.block] + self.ups + self.downs
        pieces = []
        for k in range(count):
            which = jnp.where(pos == k, 0, jnp.where(pos > k, pos - k, count - 1 + k - pos))
            pieces.append(lax.select_n(which.astype(jnp.int32), *cases))
        return jnp.concatenate(pieces, axis=0)


def run_slot(entries):
    pos = lax.axis_index("r")
    loads = [entry.payload(step) for entry, step in entries]
    ranges = [entry.senders(step) for entry, step in entries]
    received = []
    for direction, shift in ((0, 1), (1, -1)):
        combined = None
        pairs = []
        for load, rng in zip(loads, ranges):
            lo, hi = rng[direction]
            if lo > hi:
                continue
            pairs += [(i, i + shift) for i in range(lo, hi + 1)]
            mine = (pos >= lo) & (pos <= hi)
            combined = load[direction] if combined is None else jnp.where(mine, load[direction], combined)
        if combined is None:
            received.append(None)
            continue
        received.append(lax.ppermute(combined, "r", pairs))
    for (entry, step), load, rng in zip(entries, loads, ranges):
        parts = []
        for direction, shift in ((0, 1), (1, -1)):
            lo, hi = rng[direction]
            got = received[direction]
            if got is None or lo > hi:
                parts.append(jnp.zeros_like(load[direction]))
                continue
            mine = (pos >= lo + shift) & (pos <= hi + shift)
            parts.append(jnp.where(mine, got, jnp.zeros_like(got)))
        entry.receive(step, *parts)


def on_device(hidden_in, w_up, w_down, out_grad):
    up_tile = w_up[0]
    down_tile = w_down[0]
    count = lax.axis_size("r")
    x_rows = lax.all_gather(hidden_in, "p", axis=1, tiled=True)
    up_terms = jnp.dot(x_rows, up_tile, preferred_element_type=jnp.float32).astype(jnp.bfloat16)
    grad_rows = lax.all_gather(out_grad, "p", axis=1, tiled=True)
    grad_terms = lax.dot_general(
        grad_rows, down_tile, (((1,), (1,)), ((), ())), preferred_element_type=jnp.float32
    ).astype(jnp.bfloat16)

    up_sum = LineReduce(up_terms)
    if count > 1:
        run_slot([(up_sum, 0)])
        up_sum.up_in, up_sum.down_in, grad_terms = lax.optimization_barrier(
            (up_sum.up_in, up_sum.down_in, grad_terms)
        )
    grad_sum = LineReduce(grad_terms)
    for step in range(1, count - 1):
        run_slot([(up_sum, step)])
    preact = up_sum.result()
    act_gather = LineGather(gelu_value(preact).astype(jnp.bfloat16))
    if count > 1:
        run_slot([(act_gather, 0)])
    for step in range(1, count - 1):
        run_slot([(act_gather, step), (grad_sum, step - 1)])
    activation = act_gather.result()
    out_part = jnp.dot(activation, down_tile, preferred_element_type=jnp.float32)
    out_sum = lax.psum_scatter(out_part, "p", scatter_dimension=1, tiled=True)
    grad_down = lax.dot_general(
        activation, grad_rows, (((0,), (0,)), ((), ())), preferred_element_type=jnp.float32
    ).astype(jnp.bfloat16)
    if count > 1:
        run_slot([(grad_sum, count - 2)])
    act_grad = grad_sum.result()
    pre_gather = LineGather((act_grad * gelu_slope(preact)).astype(jnp.bfloat16))
    for step in range(count - 1):
        run_slot([(pre_gather, step)])
        if step == min(1, count - 2):
            pre_gather.up_cur, pre_gather.down_cur, out_sum, grad_down = lax.optimization_barrier(
                (pre_gather.up_cur, pre_gather.down_cur, out_sum, grad_down)
            )
            pre_gather.ups[-1], pre_gather.downs[-1] = pre_gather.up_cur, pre_gather.down_cur
    block_out = (hidden_in.astype(jnp.float32) + out_sum).astype(jnp.bfloat16)

    pos = lax.axis_index("r")
    rows = pre_gather.block.shape[0]
    pieces = [(pre_gather.block, pos)]
    for step in range(count - 1):
        up_piece, down_piece = pre_gather.ups[step], pre_gather.downs[step]
        up_at, down_at = pos - 1 - step, pos + 1 + step
        if 2 * step + 3 <= count:
            pieces += [(up_piece, up_at), (down_piece, down_at)]
        else:
            pieces.append((up_piece + down_piece, jnp.where(up_at >= 0, up_at, down_at)))
    sums = []
    for piece, at in pieces:
        back_rows = lax.dot_general(
            piece, up_tile, (((1,), (1,)), ((), ())), preferred_element_type=jnp.float32
        )
        sums.append((lax.psum_scatter(back_rows, "p", scatter_dimension=1, tiled=True), at))
    pre_grad = pre_gather.result()
    grad_up = lax.dot_general(
        x_rows, pre_grad, (((0,), (0,)), ((), ())), preferred_element_type=jnp.float32
    ).astype(jnp.bfloat16)
    grad_blocks = out_grad.reshape(count, rows, out_grad.shape[1]).astype(jnp.float32)
    input_rows = []
    for k in range(count):
        total = grad_blocks[k]
        for value, at in sums:
            total = total + jnp.where(at == k, value, jnp.zeros_like(value))
        input_rows.append(total)
    input_grad = jnp.concatenate(input_rows, axis=0).astype(jnp.bfloat16)
    return (block_out, input_grad, grad_up[None], grad_down[None])


def solution(mesh):
    groups = mesh.shape["groups"]
    tile = mesh.shape["tile"]

    def run(hidden_in, w_up, w_down, out_grad):
        width_blocks = hidden_in.shape[1] // w_up.shape[1]
        grid = Mesh(
            np.asarray(mesh.devices).reshape(groups, width_blocks, tile // width_blocks),
            ("groups", "r", "p"),
        )
        cells = ("r", "p")
        return jax.shard_map(
            on_device,
            mesh=grid,
            in_specs=(
                P("groups", cells),
                P(cells, None, None),
                P(cells, None, None),
                P("groups", cells),
            ),
            out_specs=(
                P("groups", cells),
                P("groups", cells),
                P(cells, "groups", None),
                P(cells, "groups", None),
            ),
            check_vma=False,
        )(hidden_in, w_up, w_down, out_grad)

    return run
```

```python
import jax
import jax.numpy as jnp
import numpy as np
from jax import lax
from jax.sharding import Mesh
from jax.sharding import PartitionSpec as P


root_half = 0.7071067811865476
inv_root_tau = 0.3989422804014327


def gelu_value(values):
    return 0.5 * values * (1.0 + lax.erf(values * root_half))


def gelu_slope(values):
    return (
        0.5 * (1.0 + lax.erf(values * root_half))
        + values * jnp.exp(-0.5 * values * values) * inv_root_tau
    )


class LineReduce:
    def __init__(self, terms):
        self.count = lax.axis_size("r")
        self.pos = lax.axis_index("r")
        rows = terms.shape[0] // self.count
        self.shares = terms.reshape(self.count, rows, terms.shape[1])
        self.up_in = jnp.zeros((rows, terms.shape[1]), jnp.float32)
        self.down_in = jnp.zeros((rows, terms.shape[1]), jnp.float32)

    def senders(self, step):
        return (0, step), (self.count - 1 - step, self.count - 1)

    def payload(self, step):
        last = self.count - 1
        up_block = jnp.clip(last - step + self.pos, 0, last)
        down_block = jnp.clip(self.pos + step - last, 0, last)
        up = self.up_in + lax.dynamic_index_in_dim(self.shares, up_block, 0, keepdims=False)
        down = self.down_in + lax.dynamic_index_in_dim(self.shares, down_block, 0, keepdims=False)
        return up.astype(jnp.bfloat16), down.astype(jnp.bfloat16)

    def receive(self, step, up, down):
        self.up_in = up.astype(jnp.float32)
        self.down_in = down.astype(jnp.float32)

    def result(self):
        own = lax.dynamic_index_in_dim(self.shares, self.pos, 0, keepdims=False)
        return self.up_in + own.astype(jnp.float32) + self.down_in


class LineGather:
    def __init__(self, block):
        self.count = lax.axis_size("r")
        self.pos = lax.axis_index("r")
        self.block = block
        self.up_cur = self.down_cur = block
        self.ups, self.downs = [], []

    def senders(self, step):
        return (step, self.count - 2), (1, self.count - 1 - step)

    def payload(self, step):
        return self.up_cur, self.down_cur

    def receive(self, step, up, down):
        self.up_cur, self.down_cur = up, down
        self.ups.append(up)
        self.downs.append(down)

    def result(self):
        count, pos = self.count, self.pos
        cases = [self.block] + self.ups + self.downs
        pieces = []
        for k in range(count):
            which = jnp.where(pos == k, 0, jnp.where(pos > k, pos - k, count - 1 + k - pos))
            pieces.append(lax.select_n(which.astype(jnp.int32), *cases))
        return jnp.concatenate(pieces, axis=0)


def run_slot(entries):
    pos = lax.axis_index("r")
    loads = [entry.payload(step) for entry, step in entries]
    ranges = [entry.senders(step) for entry, step in entries]
    received = []
    for direction, shift in ((0, 1), (1, -1)):
        combined = None
        pairs = []
        for load, rng in zip(loads, ranges):
            lo, hi = rng[direction]
            if lo > hi:
                continue
            pairs += [(i, i + shift) for i in range(lo, hi + 1)]
            mine = (pos >= lo) & (pos <= hi)
            combined = load[direction] if combined is None else jnp.where(mine, load[direction], combined)
        if combined is None:
            received.append(None)
            continue
        received.append(lax.ppermute(combined, "r", pairs))
    for (entry, step), load, rng in zip(entries, loads, ranges):
        parts = []
        for direction, shift in ((0, 1), (1, -1)):
            lo, hi = rng[direction]
            got = received[direction]
            if got is None or lo > hi:
                parts.append(jnp.zeros_like(load[direction]))
                continue
            mine = (pos >= lo + shift) & (pos <= hi + shift)
            parts.append(jnp.where(mine, got, jnp.zeros_like(got)))
        entry.receive(step, *parts)


def on_device(hidden_in, w_up, w_down, out_grad):
    up_tile = w_up[0]
    down_tile = w_down[0]
    count = lax.axis_size("r")
    x_rows = lax.all_gather(hidden_in, "p", axis=1, tiled=True)
    up_terms = jnp.dot(x_rows, up_tile, preferred_element_type=jnp.float32).astype(jnp.bfloat16)
    grad_rows = lax.all_gather(out_grad, "p", axis=1, tiled=True)
    grad_terms = lax.dot_general(
        grad_rows, down_tile, (((1,), (1,)), ((), ())), preferred_element_type=jnp.float32
    ).astype(jnp.bfloat16)

    up_sum = LineReduce(up_terms)
    if count > 1:
        run_slot([(up_sum, 0)])
        up_sum.up_in, up_sum.down_in, grad_terms = lax.optimization_barrier(
            (up_sum.up_in, up_sum.down_in, grad_terms)
        )
    grad_sum = LineReduce(grad_terms)
    for step in range(1, count - 1):
        run_slot([(up_sum, step)])
    preact = up_sum.result()
    act_shard = gelu_value(preact).astype(jnp.bfloat16)
    act_shard, grad_sum.shares = lax.optimization_barrier((act_shard, grad_sum.shares))
    activation = lax.all_gather(act_shard, "r", axis=0, tiled=True)
    for step in range(count - 1):
        run_slot([(grad_sum, step)])
    out_part = jnp.dot(activation, down_tile, preferred_element_type=jnp.float32)
    out_sum = lax.psum_scatter(out_part, "p", scatter_dimension=1, tiled=True)
    grad_down = lax.dot_general(
        activation, grad_rows, (((0,), (0,)), ((), ())), preferred_element_type=jnp.float32
    ).astype(jnp.bfloat16)
    act_grad = grad_sum.result()
    pre_grad = lax.all_gather(
        (act_grad * gelu_slope(preact)).astype(jnp.bfloat16), "r", axis=0, tiled=True
    )
    block_out = (hidden_in.astype(jnp.float32) + out_sum).astype(jnp.bfloat16)
    grad_up = lax.dot_general(
        x_rows, pre_grad, (((0,), (0,)), ((), ())), preferred_element_type=jnp.float32
    ).astype(jnp.bfloat16)
    back_part = lax.dot_general(
        pre_grad, up_tile, (((1,), (1,)), ((), ())), preferred_element_type=jnp.float32
    )
    input_grad = (
        out_grad.astype(jnp.float32)
        + lax.psum_scatter(back_part, "p", scatter_dimension=1, tiled=True)
    ).astype(jnp.bfloat16)
    return (block_out, input_grad, grad_up[None], grad_down[None])


def solution(mesh):
    groups = mesh.shape["groups"]
    tile = mesh.shape["tile"]

    def run(hidden_in, w_up, w_down, out_grad):
        width_blocks = hidden_in.shape[1] // w_up.shape[1]
        grid = Mesh(
            np.asarray(mesh.devices).reshape(groups, width_blocks, tile // width_blocks),
            ("groups", "r", "p"),
        )
        cells = ("r", "p")
        return jax.shard_map(
            on_device,
            mesh=grid,
            in_specs=(
                P("groups", cells),
                P(cells, None, None),
                P(cells, None, None),
                P("groups", cells),
            ),
            out_specs=(
                P("groups", cells),
                P("groups", cells),
                P(cells, "groups", None),
                P(cells, "groups", None),
            ),
            check_vma=False,
        )(hidden_in, w_up, w_down, out_grad)

    return run
```

```python
import jax
import jax.numpy as jnp
import numpy as np
from jax import lax
from jax.sharding import Mesh
from jax.sharding import PartitionSpec as P


root_half = 0.7071067811865476
inv_root_tau = 0.3989422804014327


def gelu_value(values):
    return 0.5 * values * (1.0 + lax.erf(values * root_half))


def gelu_slope(values):
    return (
        0.5 * (1.0 + lax.erf(values * root_half))
        + values * jnp.exp(-0.5 * values * values) * inv_root_tau
    )


class LineReduce:
    def __init__(self, terms):
        self.count = lax.axis_size("r")
        self.pos = lax.axis_index("r")
        rows = terms.shape[0] // self.count
        self.shares = terms.reshape(self.count, rows, terms.shape[1])
        self.up_in = jnp.zeros((rows, terms.shape[1]), jnp.float32)
        self.down_in = jnp.zeros((rows, terms.shape[1]), jnp.float32)

    def senders(self, step):
        return (0, step), (self.count - 1 - step, self.count - 1)

    def payload(self, step):
        last = self.count - 1
        up_block = jnp.clip(last - step + self.pos, 0, last)
        down_block = jnp.clip(self.pos + step - last, 0, last)
        up = self.up_in + lax.dynamic_index_in_dim(self.shares, up_block, 0, keepdims=False)
        down = self.down_in + lax.dynamic_index_in_dim(self.shares, down_block, 0, keepdims=False)
        return up.astype(jnp.bfloat16), down.astype(jnp.bfloat16)

    def receive(self, step, up, down):
        self.up_in = up.astype(jnp.float32)
        self.down_in = down.astype(jnp.float32)

    def result(self):
        own = lax.dynamic_index_in_dim(self.shares, self.pos, 0, keepdims=False)
        return self.up_in + own.astype(jnp.float32) + self.down_in


class LineGather:
    def __init__(self, block):
        self.count = lax.axis_size("r")
        self.pos = lax.axis_index("r")
        self.block = block
        self.up_cur = self.down_cur = block
        self.ups, self.downs = [], []

    def senders(self, step):
        return (step, self.count - 2), (1, self.count - 1 - step)

    def payload(self, step):
        return self.up_cur, self.down_cur

    def receive(self, step, up, down):
        self.up_cur, self.down_cur = up, down
        self.ups.append(up)
        self.downs.append(down)

    def result(self):
        count = self.count
        pieces = [self.block]
        for m in range(1, count):
            pieces.append(self.downs[m - 1] + self.ups[count - 1 - m])
        return jnp.concatenate(pieces, axis=0)


def rotate_rows(values, shift):
    doubled = jnp.concatenate([values, values], axis=0)
    return lax.dynamic_slice_in_dim(doubled, shift, values.shape[0], axis=0)


def run_slot(entries):
    pos = lax.axis_index("r")
    loads = [entry.payload(step) for entry, step in entries]
    ranges = [entry.senders(step) for entry, step in entries]
    received = []
    for direction, shift in ((0, 1), (1, -1)):
        combined = None
        pairs = []
        for load, rng in zip(loads, ranges):
            lo, hi = rng[direction]
            if lo > hi:
                continue
            pairs += [(i, i + shift) for i in range(lo, hi + 1)]
            mine = (pos >= lo) & (pos <= hi)
            combined = load[direction] if combined is None else jnp.where(mine, load[direction], combined)
        if combined is None:
            received.append(None)
            continue
        received.append(lax.ppermute(combined, "r", pairs))
    for (entry, step), load, rng in zip(entries, loads, ranges):
        parts = []
        for direction, shift in ((0, 1), (1, -1)):
            lo, hi = rng[direction]
            got = received[direction]
            if got is None or lo > hi:
                parts.append(jnp.zeros_like(load[direction]))
                continue
            mine = (pos >= lo + shift) & (pos <= hi + shift)
            parts.append(jnp.where(mine, got, jnp.zeros_like(got)))
        entry.receive(step, *parts)


def on_device(hidden_in, w_up, w_down, out_grad):
    up_tile = w_up[0]
    down_tile = w_down[0]
    count = lax.axis_size("r")
    x_rows = lax.all_gather(hidden_in, "p", axis=1, tiled=True)
    up_terms = jnp.dot(x_rows, up_tile, preferred_element_type=jnp.float32).astype(jnp.bfloat16)
    grad_rows = lax.all_gather(out_grad, "p", axis=1, tiled=True)
    grad_terms = lax.dot_general(
        grad_rows, down_tile, (((1,), (1,)), ((), ())), preferred_element_type=jnp.float32
    ).astype(jnp.bfloat16)

    up_sum = LineReduce(up_terms)
    if count > 1:
        run_slot([(up_sum, 0)])
        up_sum.up_in, up_sum.down_in, grad_terms = lax.optimization_barrier(
            (up_sum.up_in, up_sum.down_in, grad_terms)
        )
    grad_sum = LineReduce(grad_terms)
    for step in range(1, count - 1):
        run_slot([(up_sum, step)])
    preact = up_sum.result()
    act_gather = LineGather(gelu_value(preact).astype(jnp.bfloat16))
    if count > 1:
        run_slot([(act_gather, 0)])
    for step in range(1, count - 1):
        run_slot([(act_gather, step), (grad_sum, step - 1)])
    tokens = x_rows.shape[0]
    turn = lax.axis_index("r") * (tokens // count)
    grad_turned = rotate_rows(grad_rows, turn)
    activation = act_gather.result()
    out_part = jnp.dot(activation, down_tile, preferred_element_type=jnp.float32)
    out_sum = lax.psum_scatter(out_part, "p", scatter_dimension=1, tiled=True)
    grad_down = lax.dot_general(
        activation, grad_turned, (((0,), (0,)), ((), ())), preferred_element_type=jnp.float32
    ).astype(jnp.bfloat16)
    if count > 1:
        run_slot([(grad_sum, count - 2)])
    act_grad = grad_sum.result()
    pre_gather = LineGather((act_grad * gelu_slope(preact)).astype(jnp.bfloat16))
    for step in range(count - 1):
        run_slot([(pre_gather, step)])
        if step == min(1, count - 2):
            pre_gather.up_cur, pre_gather.down_cur, out_sum, grad_down = lax.optimization_barrier(
                (pre_gather.up_cur, pre_gather.down_cur, out_sum, grad_down)
            )
            pre_gather.ups[-1], pre_gather.downs[-1] = pre_gather.up_cur, pre_gather.down_cur
    pre_grad = pre_gather.result()
    block_out = (
        hidden_in.astype(jnp.float32) + rotate_rows(out_sum, tokens - turn)
    ).astype(jnp.bfloat16)
    grad_up = lax.dot_general(
        rotate_rows(x_rows, turn), pre_grad, (((0,), (0,)), ((), ())), preferred_element_type=jnp.float32
    ).astype(jnp.bfloat16)
    back_part = lax.dot_general(
        pre_grad, up_tile, (((1,), (1,)), ((), ())), preferred_element_type=jnp.float32
    )
    back_sum = lax.psum_scatter(back_part, "p", scatter_dimension=1, tiled=True)
    input_grad = (
        out_grad.astype(jnp.float32) + rotate_rows(back_sum, tokens - turn)
    ).astype(jnp.bfloat16)
    return (block_out, input_grad, grad_up[None], grad_down[None])


def solution(mesh):
    groups = mesh.shape["groups"]
    tile = mesh.shape["tile"]

    def run(hidden_in, w_up, w_down, out_grad):
        width_blocks = hidden_in.shape[1] // w_up.shape[1]
        grid = Mesh(
            np.asarray(mesh.devices).reshape(groups, width_blocks, tile // width_blocks),
            ("groups", "r", "p"),
        )
        cells = ("r", "p")
        return jax.shard_map(
            on_device,
            mesh=grid,
            in_specs=(
                P("groups", cells),
                P(cells, None, None),
                P(cells, None, None),
                P("groups", cells),
            ),
            out_specs=(
                P("groups", cells),
                P("groups", cells),
                P(cells, "groups", None),
                P(cells, "groups", None),
            ),
            check_vma=False,
        )(hidden_in, w_up, w_down, out_grad)

    return run
```

```python
import jax
import jax.numpy as jnp
import numpy as np
from jax import lax
from jax.sharding import Mesh
from jax.sharding import PartitionSpec as P


root_half = 0.7071067811865476
inv_root_tau = 0.3989422804014327


def gelu_value(values):
    return 0.5 * values * (1.0 + lax.erf(values * root_half))


def gelu_slope(values):
    return (
        0.5 * (1.0 + lax.erf(values * root_half))
        + values * jnp.exp(-0.5 * values * values) * inv_root_tau
    )


class LineReduce:
    def __init__(self, terms):
        self.count = lax.axis_size("r")
        self.pos = lax.axis_index("r")
        rows = terms.shape[0] // self.count
        self.shares = terms.reshape(self.count, rows, terms.shape[1])
        self.up_in = jnp.zeros((rows, terms.shape[1]), jnp.float32)
        self.down_in = jnp.zeros((rows, terms.shape[1]), jnp.float32)

    def senders(self, step):
        return (0, step), (self.count - 1 - step, self.count - 1)

    def payload(self, step):
        last = self.count - 1
        up_block = jnp.clip(last - step + self.pos, 0, last)
        down_block = jnp.clip(self.pos + step - last, 0, last)
        up = self.up_in + lax.dynamic_index_in_dim(self.shares, up_block, 0, keepdims=False)
        down = self.down_in + lax.dynamic_index_in_dim(self.shares, down_block, 0, keepdims=False)
        return up.astype(jnp.bfloat16), down.astype(jnp.bfloat16)

    def receive(self, step, up, down):
        self.up_in = up.astype(jnp.float32)
        self.down_in = down.astype(jnp.float32)

    def result(self):
        own = lax.dynamic_index_in_dim(self.shares, self.pos, 0, keepdims=False)
        return self.up_in + own.astype(jnp.float32) + self.down_in


class LineGather:
    def __init__(self, block):
        self.count = lax.axis_size("r")
        self.pos = lax.axis_index("r")
        self.block = block
        self.up_cur = self.down_cur = block
        self.ups, self.downs = [], []

    def senders(self, step):
        return (step, self.count - 2), (1, self.count - 1 - step)

    def payload(self, step):
        return self.up_cur, self.down_cur

    def receive(self, step, up, down):
        self.up_cur, self.down_cur = up, down
        self.ups.append(up)
        self.downs.append(down)

    def result(self):
        count = self.count
        pieces = [self.block]
        for m in range(1, count):
            pieces.append(self.downs[m - 1] + self.ups[count - 1 - m])
        return jnp.concatenate(pieces, axis=0)


def rotate_rows(values, shift):
    doubled = jnp.concatenate([values, values], axis=0)
    return lax.dynamic_slice_in_dim(doubled, shift, values.shape[0], axis=0)


def run_slot(entries):
    pos = lax.axis_index("r")
    loads = [entry.payload(step) for entry, step in entries]
    ranges = [entry.senders(step) for entry, step in entries]
    received = []
    for direction, shift in ((0, 1), (1, -1)):
        combined = None
        pairs = []
        for load, rng in zip(loads, ranges):
            lo, hi = rng[direction]
            if lo > hi:
                continue
            pairs += [(i, i + shift) for i in range(lo, hi + 1)]
            mine = (pos >= lo) & (pos <= hi)
            combined = load[direction] if combined is None else jnp.where(mine, load[direction], combined)
        if combined is None:
            received.append(None)
            continue
        received.append(lax.ppermute(combined, "r", pairs))
    for (entry, step), load, rng in zip(entries, loads, ranges):
        parts = []
        for direction, shift in ((0, 1), (1, -1)):
            lo, hi = rng[direction]
            got = received[direction]
            if got is None or lo > hi:
                parts.append(jnp.zeros_like(load[direction]))
                continue
            mine = (pos >= lo + shift) & (pos <= hi + shift)
            parts.append(jnp.where(mine, got, jnp.zeros_like(got)))
        entry.receive(step, *parts)


def on_device(hidden_in, w_up, w_down, out_grad):
    up_tile = w_up[0]
    down_tile = w_down[0]
    count = lax.axis_size("r")
    x_rows = lax.all_gather(hidden_in, "p", axis=1, tiled=True)
    up_terms = jnp.dot(x_rows, up_tile, preferred_element_type=jnp.float32).astype(jnp.bfloat16)
    grad_rows = lax.all_gather(out_grad, "p", axis=1, tiled=True)
    grad_terms = lax.dot_general(
        grad_rows, down_tile, (((1,), (1,)), ((), ())), preferred_element_type=jnp.float32
    ).astype(jnp.bfloat16)

    up_sum = LineReduce(up_terms)
    if count > 1:
        run_slot([(up_sum, 0)])
        up_sum.up_in, up_sum.down_in, grad_terms = lax.optimization_barrier(
            (up_sum.up_in, up_sum.down_in, grad_terms)
        )
    grad_sum = LineReduce(grad_terms)
    for step in range(1, count - 1):
        run_slot([(up_sum, step)])
    preact = up_sum.result()
    act_gather = LineGather(gelu_value(preact).astype(jnp.bfloat16))
    if count > 1:
        run_slot([(act_gather, 0)])
    for step in range(1, count - 1):
        run_slot([(act_gather, step), (grad_sum, step - 1)])
    tokens = x_rows.shape[0]
    turn = lax.axis_index("r") * (tokens // count)
    grad_turned = rotate_rows(grad_rows, turn)
    activation = act_gather.result()
    out_part = jnp.dot(activation, down_tile, preferred_element_type=jnp.float32)
    out_sum = lax.psum_scatter(out_part, "p", scatter_dimension=1, tiled=True)
    grad_down = lax.dot_general(
        activation, grad_turned, (((0,), (0,)), ((), ())), preferred_element_type=jnp.float32
    ).astype(jnp.bfloat16)
    if count > 1:
        run_slot([(grad_sum, count - 2)])
    act_grad = grad_sum.result()
    pre_gather = LineGather((act_grad * gelu_slope(preact)).astype(jnp.bfloat16))
    for step in range(count - 1):
        run_slot([(pre_gather, step)])
        if step == min(1, count - 2):
            pre_gather.up_cur, pre_gather.down_cur, out_sum, grad_down = lax.optimization_barrier(
                (pre_gather.up_cur, pre_gather.down_cur, out_sum, grad_down)
            )
            pre_gather.ups[-1], pre_gather.downs[-1] = pre_gather.up_cur, pre_gather.down_cur
    pre_grad = pre_gather.result()
    block_out = (
        hidden_in.astype(jnp.float32) + rotate_rows(out_sum, tokens - turn)
    ).astype(jnp.bfloat16)
    grad_up = lax.dot_general(
        rotate_rows(x_rows, turn), pre_grad, (((0,), (0,)), ((), ())), preferred_element_type=jnp.float32
    ).astype(jnp.bfloat16)
    pos = lax.axis_index("r")
    pieces = [(pre_gather.block, pos)]
    for step in range(count - 1):
        up_piece, down_piece = pre_gather.ups[step], pre_gather.downs[step]
        up_at, down_at = pos - 1 - step, pos + 1 + step
        if 2 * step + 3 <= count:
            pieces += [(up_piece, up_at), (down_piece, down_at)]
        else:
            pieces.append((up_piece + down_piece, jnp.where(up_at >= 0, up_at, down_at)))
    sums = []
    for piece, at in pieces:
        back_rows = lax.dot_general(
            piece, up_tile, (((1,), (1,)), ((), ())), preferred_element_type=jnp.float32
        )
        sums.append((lax.psum_scatter(back_rows, "p", scatter_dimension=1, tiled=True), at))
    rows = pre_gather.block.shape[0]
    grad_blocks = out_grad.reshape(count, rows, out_grad.shape[1]).astype(jnp.float32)
    input_rows = []
    for k in range(count):
        total = grad_blocks[k]
        for value, at in sums:
            total = total + jnp.where(at == k, value, jnp.zeros_like(value))
        input_rows.append(total)
    input_grad = jnp.concatenate(input_rows, axis=0).astype(jnp.bfloat16)
    return (block_out, input_grad, grad_up[None], grad_down[None])


def solution(mesh):
    groups = mesh.shape["groups"]
    tile = mesh.shape["tile"]

    def run(hidden_in, w_up, w_down, out_grad):
        width_blocks = hidden_in.shape[1] // w_up.shape[1]
        grid = Mesh(
            np.asarray(mesh.devices).reshape(groups, width_blocks, tile // width_blocks),
            ("groups", "r", "p"),
        )
        cells = ("r", "p")
        return jax.shard_map(
            on_device,
            mesh=grid,
            in_specs=(
                P("groups", cells),
                P(cells, None, None),
                P(cells, None, None),
                P("groups", cells),
            ),
            out_specs=(
                P("groups", cells),
                P("groups", cells),
                P(cells, "groups", None),
                P(cells, "groups", None),
            ),
            check_vma=False,
        )(hidden_in, w_up, w_down, out_grad)

    return run
```

```python
import jax
import jax.numpy as jnp
import numpy as np
from jax import lax
from jax.sharding import Mesh
from jax.sharding import PartitionSpec as P


root_half = 0.7071067811865476
inv_root_tau = 0.3989422804014327


def gelu_value(values):
    return 0.5 * values * (1.0 + lax.erf(values * root_half))


def gelu_slope(values):
    return (
        0.5 * (1.0 + lax.erf(values * root_half))
        + values * jnp.exp(-0.5 * values * values) * inv_root_tau
    )


class LineReduce:
    def __init__(self, terms):
        self.count = lax.axis_size("r")
        self.pos = lax.axis_index("r")
        rows = terms.shape[0] // self.count
        self.shares = terms.reshape(self.count, rows, terms.shape[1])
        self.up_in = jnp.zeros((rows, terms.shape[1]), jnp.float32)
        self.down_in = jnp.zeros((rows, terms.shape[1]), jnp.float32)
        self.first = None

    def senders(self, step):
        return (0, step), (self.count - 1 - step, self.count - 1)

    def payload(self, step):
        if step == 0 and self.first is not None:
            return self.first
        last = self.count - 1
        up_block = jnp.clip(last - step + self.pos, 0, last)
        down_block = jnp.clip(self.pos + step - last, 0, last)
        up = self.up_in + lax.dynamic_index_in_dim(self.shares, up_block, 0, keepdims=False)
        down = self.down_in + lax.dynamic_index_in_dim(self.shares, down_block, 0, keepdims=False)
        return up.astype(jnp.bfloat16), down.astype(jnp.bfloat16)

    def receive(self, step, up, down):
        self.up_in = up.astype(jnp.float32)
        self.down_in = down.astype(jnp.float32)

    def result(self):
        own = lax.dynamic_index_in_dim(self.shares, self.pos, 0, keepdims=False)
        return self.up_in + own.astype(jnp.float32) + self.down_in


class LineGather:
    def __init__(self, block):
        self.count = lax.axis_size("r")
        self.pos = lax.axis_index("r")
        self.block = block
        self.up_cur = self.down_cur = block
        self.ups, self.downs = [], []

    def senders(self, step):
        return (step, self.count - 2), (1, self.count - 1 - step)

    def payload(self, step):
        return self.up_cur, self.down_cur

    def receive(self, step, up, down):
        self.up_cur, self.down_cur = up, down
        self.ups.append(up)
        self.downs.append(down)

    def result(self):
        count = self.count
        pieces = [self.block]
        for m in range(1, count):
            pieces.append(self.downs[m - 1] + self.ups[count - 1 - m])
        return jnp.concatenate(pieces, axis=0)


def rotate_rows(values, shift):
    doubled = jnp.concatenate([values, values], axis=0)
    return lax.dynamic_slice_in_dim(doubled, shift, values.shape[0], axis=0)


def run_slot(entries):
    pos = lax.axis_index("r")
    loads = [entry.payload(step) for entry, step in entries]
    ranges = [entry.senders(step) for entry, step in entries]
    received = []
    for direction, shift in ((0, 1), (1, -1)):
        combined = None
        pairs = []
        for load, rng in zip(loads, ranges):
            lo, hi = rng[direction]
            if lo > hi:
                continue
            pairs += [(i, i + shift) for i in range(lo, hi + 1)]
            mine = (pos >= lo) & (pos <= hi)
            combined = load[direction] if combined is None else jnp.where(mine, load[direction], combined)
        if combined is None:
            received.append(None)
            continue
        received.append(lax.ppermute(combined, "r", pairs))
    for (entry, step), load, rng in zip(entries, loads, ranges):
        parts = []
        for direction, shift in ((0, 1), (1, -1)):
            lo, hi = rng[direction]
            got = received[direction]
            if got is None or lo > hi:
                parts.append(jnp.zeros_like(load[direction]))
                continue
            mine = (pos >= lo + shift) & (pos <= hi + shift)
            parts.append(jnp.where(mine, got, jnp.zeros_like(got)))
        entry.receive(step, *parts)


def on_device(hidden_in, w_up, w_down, out_grad):
    up_tile = w_up[0]
    down_tile = w_down[0]
    count = lax.axis_size("r")
    x_rows = lax.all_gather(hidden_in, "p", axis=1, tiled=True)
    up_terms = jnp.dot(x_rows, up_tile, preferred_element_type=jnp.float32).astype(jnp.bfloat16)
    grad_rows = lax.all_gather(out_grad, "p", axis=1, tiled=True)
    grad_terms = lax.dot_general(
        grad_rows, down_tile, (((1,), (1,)), ((), ())), preferred_element_type=jnp.float32
    ).astype(jnp.bfloat16)

    up_sum = LineReduce(up_terms)
    if count > 1:
        rows = x_rows.shape[0] // count
        last = count - 1
        pos = lax.axis_index("r")

        def block_terms(block):
            x_block = lax.dynamic_slice_in_dim(x_rows, block * rows, rows, axis=0)
            return jnp.dot(x_block, up_tile, preferred_element_type=jnp.float32).astype(jnp.bfloat16)

        up_sum.first = (block_terms(jnp.clip(last + pos, 0, last)), block_terms(jnp.clip(pos - last, 0, last)))
        run_slot([(up_sum, 0)])
        up_sum.up_in, up_sum.down_in, up_sum.shares, grad_terms = lax.optimization_barrier(
            (up_sum.up_in, up_sum.down_in, up_sum.shares, grad_terms)
        )
    grad_sum = LineReduce(grad_terms)
    for step in range(1, count - 1):
        run_slot([(up_sum, step)])
    preact = up_sum.result()
    act_gather = LineGather(gelu_value(preact).astype(jnp.bfloat16))
    if count > 1:
        run_slot([(act_gather, 0)])
    for step in range(1, count - 1):
        run_slot([(act_gather, step), (grad_sum, step - 1)])
    tokens = x_rows.shape[0]
    turn = lax.axis_index("r") * (tokens // count)
    grad_turned = rotate_rows(grad_rows, turn)
    activation = act_gather.result()
    out_part = jnp.dot(activation, down_tile, preferred_element_type=jnp.float32)
    out_sum = lax.psum_scatter(out_part, "p", scatter_dimension=1, tiled=True)
    grad_down = lax.dot_general(
        activation, grad_turned, (((0,), (0,)), ((), ())), preferred_element_type=jnp.float32
    ).astype(jnp.bfloat16)
    if count > 1:
        run_slot([(grad_sum, count - 2)])
    act_grad = grad_sum.result()
    pre_gather = LineGather((act_grad * gelu_slope(preact)).astype(jnp.bfloat16))
    for step in range(count - 1):
        run_slot([(pre_gather, step)])
        if step == min(1, count - 2):
            pre_gather.up_cur, pre_gather.down_cur, out_sum, grad_down = lax.optimization_barrier(
                (pre_gather.up_cur, pre_gather.down_cur, out_sum, grad_down)
            )
            pre_gather.ups[-1], pre_gather.downs[-1] = pre_gather.up_cur, pre_gather.down_cur
    pre_grad = pre_gather.result()
    block_out = (
        hidden_in.astype(jnp.float32) + rotate_rows(out_sum, tokens - turn)
    ).astype(jnp.bfloat16)
    grad_up = lax.dot_general(
        rotate_rows(x_rows, turn), pre_grad, (((0,), (0,)), ((), ())), preferred_element_type=jnp.float32
    ).astype(jnp.bfloat16)
    pos = lax.axis_index("r")
    pieces = [(pre_gather.block, pos)]
    for step in range(count - 1):
        up_piece, down_piece = pre_gather.ups[step], pre_gather.downs[step]
        up_at, down_at = pos - 1 - step, pos + 1 + step
        if 2 * step + 3 <= count:
            pieces += [(up_piece, up_at), (down_piece, down_at)]
        else:
            pieces.append((up_piece + down_piece, jnp.where(up_at >= 0, up_at, down_at)))
    sums = []
    for piece, at in pieces:
        back_rows = lax.dot_general(
            piece, up_tile, (((1,), (1,)), ((), ())), preferred_element_type=jnp.float32
        )
        sums.append((lax.psum_scatter(back_rows, "p", scatter_dimension=1, tiled=True), at))
    rows = pre_gather.block.shape[0]
    grad_blocks = out_grad.reshape(count, rows, out_grad.shape[1]).astype(jnp.float32)
    input_rows = []
    for k in range(count):
        total = grad_blocks[k]
        for value, at in sums:
            total = total + jnp.where(at == k, value, jnp.zeros_like(value))
        input_rows.append(total)
    input_grad = jnp.concatenate(input_rows, axis=0).astype(jnp.bfloat16)
    return (block_out, input_grad, grad_up[None], grad_down[None])


def solution(mesh):
    groups = mesh.shape["groups"]
    tile = mesh.shape["tile"]

    def run(hidden_in, w_up, w_down, out_grad):
        width_blocks = hidden_in.shape[1] // w_up.shape[1]
        grid = Mesh(
            np.asarray(mesh.devices).reshape(groups, width_blocks, tile // width_blocks),
            ("groups", "r", "p"),
        )
        cells = ("r", "p")
        return jax.shard_map(
            on_device,
            mesh=grid,
            in_specs=(
                P("groups", cells),
                P(cells, None, None),
                P(cells, None, None),
                P("groups", cells),
            ),
            out_specs=(
                P("groups", cells),
                P("groups", cells),
                P(cells, "groups", None),
                P(cells, "groups", None),
            ),
            check_vma=False,
        )(hidden_in, w_up, w_down, out_grad)

    return run
```

```python
import jax
import jax.numpy as jnp
import numpy as np
from jax import lax
from jax.sharding import Mesh
from jax.sharding import PartitionSpec as P


root_half = 0.7071067811865476
inv_root_tau = 0.3989422804014327


def gelu_value(values):
    return 0.5 * values * (1.0 + lax.erf(values * root_half))


def gelu_slope(values):
    return (
        0.5 * (1.0 + lax.erf(values * root_half))
        + values * jnp.exp(-0.5 * values * values) * inv_root_tau
    )


class LineReduce:
    def __init__(self, terms):
        self.count = lax.axis_size("r")
        self.pos = lax.axis_index("r")
        rows = terms.shape[0] // self.count
        self.shares = terms.reshape(self.count, rows, terms.shape[1])
        self.up_in = jnp.zeros((rows, terms.shape[1]), jnp.float32)
        self.down_in = jnp.zeros((rows, terms.shape[1]), jnp.float32)
        self.first = None

    def senders(self, step):
        return (0, step), (self.count - 1 - step, self.count - 1)

    def payload(self, step):
        if step == 0 and self.first is not None:
            return self.first
        last = self.count - 1
        up_block = jnp.clip(last - step + self.pos, 0, last)
        down_block = jnp.clip(self.pos + step - last, 0, last)
        up = self.up_in + lax.dynamic_index_in_dim(self.shares, up_block, 0, keepdims=False)
        down = self.down_in + lax.dynamic_index_in_dim(self.shares, down_block, 0, keepdims=False)
        return up.astype(jnp.bfloat16), down.astype(jnp.bfloat16)

    def receive(self, step, up, down):
        self.up_in = up.astype(jnp.float32)
        self.down_in = down.astype(jnp.float32)

    def result(self):
        own = lax.dynamic_index_in_dim(self.shares, self.pos, 0, keepdims=False)
        return self.up_in + own.astype(jnp.float32) + self.down_in


class LineGather:
    def __init__(self, block):
        self.count = lax.axis_size("r")
        self.pos = lax.axis_index("r")
        self.block = block
        self.up_cur = self.down_cur = block
        self.ups, self.downs = [], []

    def senders(self, step):
        return (step, self.count - 2), (1, self.count - 1 - step)

    def payload(self, step):
        return self.up_cur, self.down_cur

    def receive(self, step, up, down):
        self.up_cur, self.down_cur = up, down
        self.ups.append(up)
        self.downs.append(down)

    def result(self):
        count = self.count
        pieces = [self.block]
        for m in range(1, count):
            pieces.append(self.downs[m - 1] + self.ups[count - 1 - m])
        return jnp.concatenate(pieces, axis=0)


def rotate_rows(values, shift):
    doubled = jnp.concatenate([values, values], axis=0)
    return lax.dynamic_slice_in_dim(doubled, shift, values.shape[0], axis=0)


def run_slot(entries):
    pos = lax.axis_index("r")
    loads = [entry.payload(step) for entry, step in entries]
    ranges = [entry.senders(step) for entry, step in entries]
    received = []
    for direction, shift in ((0, 1), (1, -1)):
        combined = None
        pairs = []
        for load, rng in zip(loads, ranges):
            lo, hi = rng[direction]
            if lo > hi:
                continue
            pairs += [(i, i + shift) for i in range(lo, hi + 1)]
            mine = (pos >= lo) & (pos <= hi)
            combined = load[direction] if combined is None else jnp.where(mine, load[direction], combined)
        if combined is None:
            received.append(None)
            continue
        received.append(lax.ppermute(combined, "r", pairs))
    for (entry, step), load, rng in zip(entries, loads, ranges):
        parts = []
        for direction, shift in ((0, 1), (1, -1)):
            lo, hi = rng[direction]
            got = received[direction]
            if got is None or lo > hi:
                parts.append(jnp.zeros_like(load[direction]))
                continue
            mine = (pos >= lo + shift) & (pos <= hi + shift)
            parts.append(jnp.where(mine, got, jnp.zeros_like(got)))
        entry.receive(step, *parts)


def on_device(hidden_in, w_up, w_down, out_grad):
    up_tile = w_up[0]
    down_tile = w_down[0]
    count = lax.axis_size("r")
    x_rows = lax.all_gather(hidden_in, "p", axis=1, tiled=True)
    up_terms = jnp.dot(x_rows, up_tile, preferred_element_type=jnp.float32).astype(jnp.bfloat16)
    grad_rows = lax.all_gather(out_grad, "p", axis=1, tiled=True)
    grad_terms = lax.dot_general(
        grad_rows, down_tile, (((1,), (1,)), ((), ())), preferred_element_type=jnp.float32
    ).astype(jnp.bfloat16)

    up_sum = LineReduce(up_terms)
    if count > 1:
        rows = x_rows.shape[0] // count
        last = count - 1
        pos = lax.axis_index("r")

        def block_terms(block):
            x_block = lax.dynamic_slice_in_dim(x_rows, block * rows, rows, axis=0)
            return jnp.dot(x_block, up_tile, preferred_element_type=jnp.float32).astype(jnp.bfloat16)

        up_sum.first = (block_terms(jnp.clip(last + pos, 0, last)), block_terms(jnp.clip(pos - last, 0, last)))
        run_slot([(up_sum, 0)])
        up_sum.up_in, up_sum.down_in, up_sum.shares, grad_terms = lax.optimization_barrier(
            (up_sum.up_in, up_sum.down_in, up_sum.shares, grad_terms)
        )
    grad_sum = LineReduce(grad_terms)
    for step in range(1, count - 1):
        run_slot([(up_sum, step)])
    preact = up_sum.result()
    act_gather = LineGather(gelu_value(preact).astype(jnp.bfloat16))
    if count > 1:
        run_slot([(act_gather, 0)])
    for step in range(1, count - 1):
        run_slot([(act_gather, step), (grad_sum, step - 1)])
    tokens = x_rows.shape[0]
    turn = lax.axis_index("r") * (tokens // count)
    grad_turned = rotate_rows(grad_rows, turn)
    activation = act_gather.result()
    out_part = jnp.dot(activation, down_tile, preferred_element_type=jnp.float32)
    grad_down = lax.dot_general(
        activation, grad_turned, (((0,), (0,)), ((), ())), preferred_element_type=jnp.float32
    ).astype(jnp.bfloat16)
    if count > 1:
        run_slot([(grad_sum, count - 2)])
        grad_sum.up_in, grad_sum.down_in, out_part = lax.optimization_barrier(
            (grad_sum.up_in, grad_sum.down_in, out_part)
        )
    out_sum = lax.psum_scatter(out_part, "p", scatter_dimension=1, tiled=True)
    act_grad = grad_sum.result()
    pre_gather = LineGather((act_grad * gelu_slope(preact)).astype(jnp.bfloat16))
    for step in range(count - 1):
        run_slot([(pre_gather, step)])
        if step == min(1, count - 2):
            pre_gather.up_cur, pre_gather.down_cur, out_sum, grad_down = lax.optimization_barrier(
                (pre_gather.up_cur, pre_gather.down_cur, out_sum, grad_down)
            )
            pre_gather.ups[-1], pre_gather.downs[-1] = pre_gather.up_cur, pre_gather.down_cur
    pre_grad = pre_gather.result()
    block_out = (
        hidden_in.astype(jnp.float32) + rotate_rows(out_sum, tokens - turn)
    ).astype(jnp.bfloat16)
    grad_up = lax.dot_general(
        rotate_rows(x_rows, turn), pre_grad, (((0,), (0,)), ((), ())), preferred_element_type=jnp.float32
    ).astype(jnp.bfloat16)
    pos = lax.axis_index("r")
    pieces = [(pre_gather.block, pos)]
    for step in range(count - 1):
        up_piece, down_piece = pre_gather.ups[step], pre_gather.downs[step]
        up_at, down_at = pos - 1 - step, pos + 1 + step
        if 2 * step + 3 <= count:
            pieces += [(up_piece, up_at), (down_piece, down_at)]
        else:
            pieces.append((up_piece + down_piece, jnp.where(up_at >= 0, up_at, down_at)))
    sums = []
    for piece, at in pieces:
        back_rows = lax.dot_general(
            piece, up_tile, (((1,), (1,)), ((), ())), preferred_element_type=jnp.float32
        )
        sums.append((lax.psum_scatter(back_rows, "p", scatter_dimension=1, tiled=True), at))
    rows = pre_gather.block.shape[0]
    grad_blocks = out_grad.reshape(count, rows, out_grad.shape[1]).astype(jnp.float32)
    input_rows = []
    for k in range(count):
        total = grad_blocks[k]
        for value, at in sums:
            total = total + jnp.where(at == k, value, jnp.zeros_like(value))
        input_rows.append(total)
    input_grad = jnp.concatenate(input_rows, axis=0).astype(jnp.bfloat16)
    return (block_out, input_grad, grad_up[None], grad_down[None])


def solution(mesh):
    groups = mesh.shape["groups"]
    tile = mesh.shape["tile"]

    def run(hidden_in, w_up, w_down, out_grad):
        width_blocks = hidden_in.shape[1] // w_up.shape[1]
        grid = Mesh(
            np.asarray(mesh.devices).reshape(groups, width_blocks, tile // width_blocks),
            ("groups", "r", "p"),
        )
        cells = ("r", "p")
        return jax.shard_map(
            on_device,
            mesh=grid,
            in_specs=(
                P("groups", cells),
                P(cells, None, None),
                P(cells, None, None),
                P("groups", cells),
            ),
            out_specs=(
                P("groups", cells),
                P("groups", cells),
                P(cells, "groups", None),
                P(cells, "groups", None),
            ),
            check_vma=False,
        )(hidden_in, w_up, w_down, out_grad)

    return run
```

```python
import jax
import jax.numpy as jnp
import numpy as np
from jax import lax
from jax.sharding import Mesh
from jax.sharding import PartitionSpec as P


root_half = 0.7071067811865476
inv_root_tau = 0.3989422804014327


def gelu_value(values):
    return 0.5 * values * (1.0 + lax.erf(values * root_half))


def gelu_slope(values):
    return (
        0.5 * (1.0 + lax.erf(values * root_half))
        + values * jnp.exp(-0.5 * values * values) * inv_root_tau
    )


class LineReduce:
    def __init__(self, terms):
        self.count = lax.axis_size("r")
        self.pos = lax.axis_index("r")
        rows = terms.shape[0] // self.count
        self.shares = terms.reshape(self.count, rows, terms.shape[1])
        self.up_in = jnp.zeros((rows, terms.shape[1]), jnp.float32)
        self.down_in = jnp.zeros((rows, terms.shape[1]), jnp.float32)
        self.first = None

    def senders(self, step):
        return (0, step), (self.count - 1 - step, self.count - 1)

    def payload(self, step):
        if step == 0 and self.first is not None:
            return self.first
        last = self.count - 1
        up_block = jnp.clip(last - step + self.pos, 0, last)
        down_block = jnp.clip(self.pos + step - last, 0, last)
        up = self.up_in + lax.dynamic_index_in_dim(self.shares, up_block, 0, keepdims=False)
        down = self.down_in + lax.dynamic_index_in_dim(self.shares, down_block, 0, keepdims=False)
        return up.astype(jnp.bfloat16), down.astype(jnp.bfloat16)

    def receive(self, step, up, down):
        self.up_in = up.astype(jnp.float32)
        self.down_in = down.astype(jnp.float32)

    def result(self):
        own = lax.dynamic_index_in_dim(self.shares, self.pos, 0, keepdims=False)
        return self.up_in + own.astype(jnp.float32) + self.down_in


class LineGather:
    def __init__(self, block):
        self.count = lax.axis_size("r")
        self.pos = lax.axis_index("r")
        self.block = block
        self.up_cur = self.down_cur = block
        self.ups, self.downs = [], []

    def senders(self, step):
        return (step, self.count - 2), (1, self.count - 1 - step)

    def payload(self, step):
        return self.up_cur, self.down_cur

    def receive(self, step, up, down):
        self.up_cur, self.down_cur = up, down
        self.ups.append(up)
        self.downs.append(down)

    def result(self):
        count = self.count
        pieces = [self.block]
        for m in range(1, count):
            pieces.append(self.downs[m - 1] + self.ups[count - 1 - m])
        return jnp.concatenate(pieces, axis=0)


def rotate_rows(values, shift):
    doubled = jnp.concatenate([values, values], axis=0)
    return lax.dynamic_slice_in_dim(doubled, shift, values.shape[0], axis=0)


def run_slot(entries):
    pos = lax.axis_index("r")
    loads = [entry.payload(step) for entry, step in entries]
    ranges = [entry.senders(step) for entry, step in entries]
    received = []
    for direction, shift in ((0, 1), (1, -1)):
        combined = None
        pairs = []
        for load, rng in zip(loads, ranges):
            lo, hi = rng[direction]
            if lo > hi:
                continue
            pairs += [(i, i + shift) for i in range(lo, hi + 1)]
            mine = (pos >= lo) & (pos <= hi)
            combined = load[direction] if combined is None else jnp.where(mine, load[direction], combined)
        if combined is None:
            received.append(None)
            continue
        received.append(lax.ppermute(combined, "r", pairs))
    for (entry, step), load, rng in zip(entries, loads, ranges):
        parts = []
        for direction, shift in ((0, 1), (1, -1)):
            lo, hi = rng[direction]
            got = received[direction]
            if got is None or lo > hi:
                parts.append(jnp.zeros_like(load[direction]))
                continue
            mine = (pos >= lo + shift) & (pos <= hi + shift)
            parts.append(jnp.where(mine, got, jnp.zeros_like(got)))
        entry.receive(step, *parts)


def on_device(hidden_in, w_up, w_down, out_grad):
    up_tile = w_up[0]
    down_tile = w_down[0]
    count = lax.axis_size("r")
    x_rows = lax.all_gather(hidden_in, "p", axis=1, tiled=True)
    up_terms = jnp.dot(x_rows, up_tile, preferred_element_type=jnp.float32).astype(jnp.bfloat16)
    grad_rows = lax.all_gather(out_grad, "p", axis=1, tiled=True)
    grad_terms = lax.dot_general(
        grad_rows, down_tile, (((1,), (1,)), ((), ())), preferred_element_type=jnp.float32
    ).astype(jnp.bfloat16)

    up_sum = LineReduce(up_terms)
    if count > 1:
        rows = x_rows.shape[0] // count
        last = count - 1
        pos = lax.axis_index("r")

        first_rows = jnp.concatenate(
            [
                lax.dynamic_slice_in_dim(x_rows, jnp.clip(last + pos, 0, last) * rows, rows, axis=0),
                lax.dynamic_slice_in_dim(x_rows, jnp.clip(pos - last, 0, last) * rows, rows, axis=0),
            ],
            axis=0,
        )
        first = jnp.dot(first_rows, up_tile, preferred_element_type=jnp.float32).astype(jnp.bfloat16)
        up_sum.first = (first[:rows], first[rows:])
        run_slot([(up_sum, 0)])
        up_sum.up_in, up_sum.down_in, up_sum.shares, grad_terms = lax.optimization_barrier(
            (up_sum.up_in, up_sum.down_in, up_sum.shares, grad_terms)
        )
    grad_sum = LineReduce(grad_terms)
    for step in range(1, count - 1):
        run_slot([(up_sum, step)])
    preact = up_sum.result()
    act_gather = LineGather(gelu_value(preact).astype(jnp.bfloat16))
    if count > 1:
        run_slot([(act_gather, 0)])
    slope = gelu_slope(preact)
    for step in range(1, count - 1):
        run_slot([(act_gather, step), (grad_sum, step - 1)])
        if step == 1:
            grad_sum.up_in, grad_sum.down_in, slope = lax.optimization_barrier(
                (grad_sum.up_in, grad_sum.down_in, slope)
            )
    tokens = x_rows.shape[0]
    turn = lax.axis_index("r") * (tokens // count)
    grad_turned = rotate_rows(grad_rows, turn)
    activation = act_gather.result()
    out_part = jnp.dot(activation, down_tile, preferred_element_type=jnp.float32)
    grad_down = lax.dot_general(
        activation, grad_turned, (((0,), (0,)), ((), ())), preferred_element_type=jnp.float32
    ).astype(jnp.bfloat16)
    if count > 1:
        run_slot([(grad_sum, count - 2)])
        grad_sum.up_in, grad_sum.down_in, out_part = lax.optimization_barrier(
            (grad_sum.up_in, grad_sum.down_in, out_part)
        )
    out_sum = lax.psum_scatter(out_part, "p", scatter_dimension=1, tiled=True)
    act_grad = grad_sum.result()
    pre_gather = LineGather((act_grad * slope).astype(jnp.bfloat16))
    for step in range(count - 1):
        run_slot([(pre_gather, step)])
        if step == min(1, count - 2):
            pre_gather.up_cur, pre_gather.down_cur, out_sum, grad_down = lax.optimization_barrier(
                (pre_gather.up_cur, pre_gather.down_cur, out_sum, grad_down)
            )
            pre_gather.ups[-1], pre_gather.downs[-1] = pre_gather.up_cur, pre_gather.down_cur
    pre_grad = pre_gather.result()
    block_out = (
        hidden_in.astype(jnp.float32) + rotate_rows(out_sum, tokens - turn)
    ).astype(jnp.bfloat16)
    grad_up = lax.dot_general(
        rotate_rows(x_rows, turn), pre_grad, (((0,), (0,)), ((), ())), preferred_element_type=jnp.float32
    ).astype(jnp.bfloat16)
    pos = lax.axis_index("r")
    pieces = [(pre_gather.block, pos)]
    for step in range(count - 1):
        up_piece, down_piece = pre_gather.ups[step], pre_gather.downs[step]
        up_at, down_at = pos - 1 - step, pos + 1 + step
        if 2 * step + 3 <= count:
            pieces += [(up_piece, up_at), (down_piece, down_at)]
        else:
            pieces.append((up_piece + down_piece, jnp.where(up_at >= 0, up_at, down_at)))
    sums = []
    for piece, at in pieces:
        back_rows = lax.dot_general(
            piece, up_tile, (((1,), (1,)), ((), ())), preferred_element_type=jnp.float32
        )
        sums.append((lax.psum_scatter(back_rows, "p", scatter_dimension=1, tiled=True), at))
    rows = pre_gather.block.shape[0]
    grad_blocks = out_grad.reshape(count, rows, out_grad.shape[1]).astype(jnp.float32)
    input_rows = []
    for k in range(count):
        total = grad_blocks[k]
        for value, at in sums:
            total = total + jnp.where(at == k, value, jnp.zeros_like(value))
        input_rows.append(total)
    input_grad = jnp.concatenate(input_rows, axis=0).astype(jnp.bfloat16)
    return (block_out, input_grad, grad_up[None], grad_down[None])


def solution(mesh):
    groups = mesh.shape["groups"]
    tile = mesh.shape["tile"]

    def run(hidden_in, w_up, w_down, out_grad):
        width_blocks = hidden_in.shape[1] // w_up.shape[1]
        grid = Mesh(
            np.asarray(mesh.devices).reshape(groups, width_blocks, tile // width_blocks),
            ("groups", "r", "p"),
        )
        cells = ("r", "p")
        return jax.shard_map(
            on_device,
            mesh=grid,
            in_specs=(
                P("groups", cells),
                P(cells, None, None),
                P(cells, None, None),
                P("groups", cells),
            ),
            out_specs=(
                P("groups", cells),
                P("groups", cells),
                P(cells, "groups", None),
                P(cells, "groups", None),
            ),
            check_vma=False,
        )(hidden_in, w_up, w_down, out_grad)

    return run
```

```python
import jax
import jax.numpy as jnp
import numpy as np
from jax import lax
from jax.sharding import Mesh
from jax.sharding import PartitionSpec as P


root_half = 0.7071067811865476
inv_root_tau = 0.3989422804014327


def gelu_value(values):
    return 0.5 * values * (1.0 + lax.erf(values * root_half))


def gelu_slope(values):
    return (
        0.5 * (1.0 + lax.erf(values * root_half))
        + values * jnp.exp(-0.5 * values * values) * inv_root_tau
    )


class LineReduce:
    def __init__(self, terms):
        self.count = lax.axis_size("r")
        self.pos = lax.axis_index("r")
        rows = terms.shape[0] // self.count
        self.shares = terms.reshape(self.count, rows, terms.shape[1])
        self.up_in = jnp.zeros((rows, terms.shape[1]), jnp.float32)
        self.down_in = jnp.zeros((rows, terms.shape[1]), jnp.float32)
        self.first = None

    def senders(self, step):
        return (0, step), (self.count - 1 - step, self.count - 1)

    def payload(self, step):
        if step == 0 and self.first is not None:
            return self.first
        last = self.count - 1
        up_block = jnp.clip(last - step + self.pos, 0, last)
        down_block = jnp.clip(self.pos + step - last, 0, last)
        up = self.up_in + lax.dynamic_index_in_dim(self.shares, up_block, 0, keepdims=False)
        down = self.down_in + lax.dynamic_index_in_dim(self.shares, down_block, 0, keepdims=False)
        return up.astype(jnp.bfloat16), down.astype(jnp.bfloat16)

    def receive(self, step, up, down):
        self.up_in = up.astype(jnp.float32)
        self.down_in = down.astype(jnp.float32)

    def result(self):
        own = lax.dynamic_index_in_dim(self.shares, self.pos, 0, keepdims=False)
        return self.up_in + own.astype(jnp.float32) + self.down_in


class LineGather:
    def __init__(self, block):
        self.count = lax.axis_size("r")
        self.pos = lax.axis_index("r")
        self.block = block
        self.up_cur = self.down_cur = block
        self.ups, self.downs = [], []

    def senders(self, step):
        return (step, self.count - 2), (1, self.count - 1 - step)

    def payload(self, step):
        return self.up_cur, self.down_cur

    def receive(self, step, up, down):
        self.up_cur, self.down_cur = up, down
        self.ups.append(up)
        self.downs.append(down)

    def result(self):
        count = self.count
        pieces = [self.block]
        for m in range(1, count):
            pieces.append(self.downs[m - 1] + self.ups[count - 1 - m])
        return jnp.concatenate(pieces, axis=0)


def rotate_rows(values, shift):
    doubled = jnp.concatenate([values, values], axis=0)
    return lax.dynamic_slice_in_dim(doubled, shift, values.shape[0], axis=0)


def run_slot(entries):
    pos = lax.axis_index("r")
    loads = [entry.payload(step) for entry, step in entries]
    ranges = [entry.senders(step) for entry, step in entries]
    received = []
    for direction, shift in ((0, 1), (1, -1)):
        combined = None
        pairs = []
        for load, rng in zip(loads, ranges):
            lo, hi = rng[direction]
            if lo > hi:
                continue
            pairs += [(i, i + shift) for i in range(lo, hi + 1)]
            mine = (pos >= lo) & (pos <= hi)
            combined = load[direction] if combined is None else jnp.where(mine, load[direction], combined)
        if combined is None:
            received.append(None)
            continue
        received.append(lax.ppermute(combined, "r", pairs))
    for (entry, step), load, rng in zip(entries, loads, ranges):
        parts = []
        for direction, shift in ((0, 1), (1, -1)):
            lo, hi = rng[direction]
            got = received[direction]
            if got is None or lo > hi:
                parts.append(jnp.zeros_like(load[direction]))
                continue
            mine = (pos >= lo + shift) & (pos <= hi + shift)
            parts.append(jnp.where(mine, got, jnp.zeros_like(got)))
        entry.receive(step, *parts)


def on_device(hidden_in, w_up, w_down, out_grad):
    up_tile = w_up[0]
    down_tile = w_down[0]
    count = lax.axis_size("r")
    x_rows = lax.all_gather(hidden_in, "p", axis=1, tiled=True)
    up_terms = jnp.dot(x_rows, up_tile, preferred_element_type=jnp.float32).astype(jnp.bfloat16)
    grad_rows = lax.all_gather(out_grad, "p", axis=1, tiled=True)
    grad_terms = lax.dot_general(
        grad_rows, down_tile, (((1,), (1,)), ((), ())), preferred_element_type=jnp.float32
    ).astype(jnp.bfloat16)

    up_sum = LineReduce(up_terms)
    if count > 1:
        rows = x_rows.shape[0] // count
        last = count - 1
        pos = lax.axis_index("r")

        def block_terms(block):
            x_block = lax.dynamic_slice_in_dim(x_rows, block * rows, rows, axis=0)
            return jnp.dot(x_block, up_tile, preferred_element_type=jnp.float32).astype(jnp.bfloat16)

        up_sum.first = (block_terms(jnp.clip(last + pos, 0, last)), block_terms(jnp.clip(pos - last, 0, last)))
        run_slot([(up_sum, 0)])
        up_sum.up_in, up_sum.down_in, up_sum.shares, grad_terms = lax.optimization_barrier(
            (up_sum.up_in, up_sum.down_in, up_sum.shares, grad_terms)
        )
    grad_sum = LineReduce(grad_terms)
    for step in range(1, count - 1):
        run_slot([(up_sum, step)])
    preact = up_sum.result()
    act_gather = LineGather(gelu_value(preact).astype(jnp.bfloat16))
    if count > 1:
        run_slot([(act_gather, 0)])
    slope = gelu_slope(preact)
    for step in range(1, count - 1):
        run_slot([(act_gather, step), (grad_sum, step - 1)])
        if step == 1:
            grad_sum.up_in, grad_sum.down_in, slope = lax.optimization_barrier(
                (grad_sum.up_in, grad_sum.down_in, slope)
            )
    tokens = x_rows.shape[0]
    turn = lax.axis_index("r") * (tokens // count)
    grad_turned = rotate_rows(grad_rows, turn)
    activation = act_gather.result()
    out_part = jnp.dot(activation, down_tile, preferred_element_type=jnp.float32)
    grad_down = lax.dot_general(
        activation, grad_turned, (((0,), (0,)), ((), ())), preferred_element_type=jnp.float32
    ).astype(jnp.bfloat16)
    if count > 1:
        run_slot([(grad_sum, count - 2)])
        grad_sum.up_in, grad_sum.down_in, out_part = lax.optimization_barrier(
            (grad_sum.up_in, grad_sum.down_in, out_part)
        )
    out_sum = lax.psum_scatter(out_part, "p", scatter_dimension=1, tiled=True)
    act_grad = grad_sum.result()
    pre_gather = LineGather((act_grad * slope).astype(jnp.bfloat16))
    for step in range(count - 1):
        run_slot([(pre_gather, step)])
        if step == min(1, count - 2):
            pre_gather.up_cur, pre_gather.down_cur, out_sum, grad_down = lax.optimization_barrier(
                (pre_gather.up_cur, pre_gather.down_cur, out_sum, grad_down)
            )
            pre_gather.ups[-1], pre_gather.downs[-1] = pre_gather.up_cur, pre_gather.down_cur
    pre_grad = pre_gather.result()
    block_out = (
        hidden_in.astype(jnp.float32) + rotate_rows(out_sum, tokens - turn)
    ).astype(jnp.bfloat16)
    grad_up = lax.dot_general(
        rotate_rows(x_rows, turn), pre_grad, (((0,), (0,)), ((), ())), preferred_element_type=jnp.float32
    ).astype(jnp.bfloat16)
    pos = lax.axis_index("r")
    pieces = [(pre_gather.block, pos)]
    for step in range(count - 1):
        up_piece, down_piece = pre_gather.ups[step], pre_gather.downs[step]
        up_at, down_at = pos - 1 - step, pos + 1 + step
        if 2 * step + 3 <= count:
            pieces += [(up_piece, up_at), (down_piece, down_at)]
        else:
            pieces.append((up_piece + down_piece, jnp.where(up_at >= 0, up_at, down_at)))
    sums = []
    for piece, at in pieces:
        back_rows = lax.dot_general(
            piece, up_tile, (((1,), (1,)), ((), ())), preferred_element_type=jnp.float32
        )
        sums.append((lax.psum_scatter(back_rows, "p", scatter_dimension=1, tiled=True), at))
    rows = pre_gather.block.shape[0]
    grad_blocks = out_grad.reshape(count, rows, out_grad.shape[1]).astype(jnp.float32)
    input_rows = []
    for k in range(count):
        total = grad_blocks[k]
        for value, at in sums:
            total = total + jnp.where(at == k, value, jnp.zeros_like(value))
        input_rows.append(total)
    input_grad = jnp.concatenate(input_rows, axis=0).astype(jnp.bfloat16)
    return (block_out, input_grad, grad_up[None], grad_down[None])


def solution(mesh):
    groups = mesh.shape["groups"]
    tile = mesh.shape["tile"]

    def run(hidden_in, w_up, w_down, out_grad):
        width_blocks = hidden_in.shape[1] // w_up.shape[1]
        grid = Mesh(
            np.asarray(mesh.devices).reshape(groups, width_blocks, tile // width_blocks),
            ("groups", "r", "p"),
        )
        cells = ("r", "p")
        return jax.shard_map(
            on_device,
            mesh=grid,
            in_specs=(
                P("groups", cells),
                P(cells, None, None),
                P(cells, None, None),
                P("groups", cells),
            ),
            out_specs=(
                P("groups", cells),
                P("groups", cells),
                P(cells, "groups", None),
                P(cells, "groups", None),
            ),
            check_vma=False,
        )(hidden_in, w_up, w_down, out_grad)

    return run
```

```python
import jax
import jax.numpy as jnp
import numpy as np
from jax import lax
from jax.sharding import Mesh
from jax.sharding import PartitionSpec as P


root_half = 0.7071067811865476
inv_root_tau = 0.3989422804014327


def gelu_value(values):
    return 0.5 * values * (1.0 + lax.erf(values * root_half))


def gelu_slope(values):
    return (
        0.5 * (1.0 + lax.erf(values * root_half))
        + values * jnp.exp(-0.5 * values * values) * inv_root_tau
    )


class LineReduce:
    def __init__(self, terms):
        self.count = lax.axis_size("r")
        self.pos = lax.axis_index("r")
        rows = terms.shape[0] // self.count
        self.shares = terms.reshape(self.count, rows, terms.shape[1])
        self.up_in = jnp.zeros((rows, terms.shape[1]), jnp.float32)
        self.down_in = jnp.zeros((rows, terms.shape[1]), jnp.float32)
        self.first = None

    def senders(self, step):
        return (0, step), (self.count - 1 - step, self.count - 1)

    def payload(self, step):
        if step == 0 and self.first is not None:
            return self.first
        last = self.count - 1
        up_block = jnp.clip(last - step + self.pos, 0, last)
        down_block = jnp.clip(self.pos + step - last, 0, last)
        up = self.up_in + lax.dynamic_index_in_dim(self.shares, up_block, 0, keepdims=False)
        down = self.down_in + lax.dynamic_index_in_dim(self.shares, down_block, 0, keepdims=False)
        return up.astype(jnp.bfloat16), down.astype(jnp.bfloat16)

    def receive(self, step, up, down):
        self.up_in = up.astype(jnp.float32)
        self.down_in = down.astype(jnp.float32)

    def result(self):
        own = lax.dynamic_index_in_dim(self.shares, self.pos, 0, keepdims=False)
        return self.up_in + own.astype(jnp.float32) + self.down_in


class LineGather:
    def __init__(self, block):
        self.count = lax.axis_size("r")
        self.pos = lax.axis_index("r")
        self.block = block
        self.up_cur = self.down_cur = block
        self.ups, self.downs = [], []

    def senders(self, step):
        return (step, self.count - 2), (1, self.count - 1 - step)

    def payload(self, step):
        return self.up_cur, self.down_cur

    def receive(self, step, up, down):
        self.up_cur, self.down_cur = up, down
        self.ups.append(up)
        self.downs.append(down)

    def result(self):
        count = self.count
        pieces = [self.block]
        for m in range(1, count):
            pieces.append(self.downs[m - 1] + self.ups[count - 1 - m])
        return jnp.concatenate(pieces, axis=0)


def rotate_rows(values, shift):
    doubled = jnp.concatenate([values, values], axis=0)
    return lax.dynamic_slice_in_dim(doubled, shift, values.shape[0], axis=0)


def run_slot(entries):
    pos = lax.axis_index("r")
    loads = [entry.payload(step) for entry, step in entries]
    ranges = [entry.senders(step) for entry, step in entries]
    received = []
    for direction, shift in ((0, 1), (1, -1)):
        combined = None
        pairs = []
        for load, rng in zip(loads, ranges):
            lo, hi = rng[direction]
            if lo > hi:
                continue
            pairs += [(i, i + shift) for i in range(lo, hi + 1)]
            mine = (pos >= lo) & (pos <= hi)
            combined = load[direction] if combined is None else jnp.where(mine, load[direction], combined)
        if combined is None:
            received.append(None)
            continue
        received.append(lax.ppermute(combined, "r", pairs))
    for (entry, step), load, rng in zip(entries, loads, ranges):
        parts = []
        for direction, shift in ((0, 1), (1, -1)):
            lo, hi = rng[direction]
            got = received[direction]
            if got is None or lo > hi:
                parts.append(jnp.zeros_like(load[direction]))
                continue
            mine = (pos >= lo + shift) & (pos <= hi + shift)
            parts.append(jnp.where(mine, got, jnp.zeros_like(got)))
        entry.receive(step, *parts)


def on_device(hidden_in, w_up, w_down, out_grad):
    up_tile = w_up[0]
    down_tile = w_down[0]
    count = lax.axis_size("r")
    x_rows = lax.all_gather(hidden_in, "p", axis=1, tiled=True)
    up_terms = jnp.dot(x_rows, up_tile, preferred_element_type=jnp.float32).astype(jnp.bfloat16)
    grad_rows = lax.all_gather(out_grad, "p", axis=1, tiled=True)
    grad_terms = lax.dot_general(
        grad_rows, down_tile, (((1,), (1,)), ((), ())), preferred_element_type=jnp.float32
    ).astype(jnp.bfloat16)

    up_sum = LineReduce(up_terms)
    if count > 1:
        rows = x_rows.shape[0] // count
        last = count - 1
        pos = lax.axis_index("r")

        own_rows = jnp.concatenate(
            [
                lax.dynamic_slice_in_dim(hidden_in, jnp.clip(last + pos, 0, last) * rows, rows, axis=0),
                lax.dynamic_slice_in_dim(hidden_in, jnp.clip(pos - last, 0, last) * rows, rows, axis=0),
            ],
            axis=0,
        )
        first_rows = lax.all_gather(own_rows, "p", axis=1, tiled=True)
        first = jnp.dot(first_rows, up_tile, preferred_element_type=jnp.float32).astype(jnp.bfloat16)
        up_sum.first = (first[:rows], first[rows:])
        run_slot([(up_sum, 0)])
        up_sum.up_in, up_sum.down_in, up_sum.shares, grad_terms = lax.optimization_barrier(
            (up_sum.up_in, up_sum.down_in, up_sum.shares, grad_terms)
        )
    grad_sum = LineReduce(grad_terms)
    for step in range(1, count - 1):
        run_slot([(up_sum, step)])
    preact = up_sum.result()
    act_gather = LineGather(gelu_value(preact).astype(jnp.bfloat16))
    if count > 1:
        run_slot([(act_gather, 0)])
    slope = gelu_slope(preact)
    for step in range(1, count - 1):
        run_slot([(act_gather, step), (grad_sum, step - 1)])
        if step == 1:
            grad_sum.up_in, grad_sum.down_in, slope = lax.optimization_barrier(
                (grad_sum.up_in, grad_sum.down_in, slope)
            )
    tokens = x_rows.shape[0]
    turn = lax.axis_index("r") * (tokens // count)
    grad_turned = rotate_rows(grad_rows, turn)
    activation = act_gather.result()
    out_part = jnp.dot(activation, down_tile, preferred_element_type=jnp.float32)
    grad_down = lax.dot_general(
        activation, grad_turned, (((0,), (0,)), ((), ())), preferred_element_type=jnp.float32
    ).astype(jnp.bfloat16)
    if count > 1:
        run_slot([(grad_sum, count - 2)])
        grad_sum.up_in, grad_sum.down_in, out_part = lax.optimization_barrier(
            (grad_sum.up_in, grad_sum.down_in, out_part)
        )
    out_sum = lax.psum_scatter(out_part, "p", scatter_dimension=1, tiled=True)
    act_grad = grad_sum.result()
    pre_gather = LineGather((act_grad * slope).astype(jnp.bfloat16))
    for step in range(count - 1):
        run_slot([(pre_gather, step)])
        if step == min(1, count - 2):
            pre_gather.up_cur, pre_gather.down_cur, out_sum, grad_down = lax.optimization_barrier(
                (pre_gather.up_cur, pre_gather.down_cur, out_sum, grad_down)
            )
            pre_gather.ups[-1], pre_gather.downs[-1] = pre_gather.up_cur, pre_gather.down_cur
    pre_grad = pre_gather.result()
    block_out = (
        hidden_in.astype(jnp.float32) + rotate_rows(out_sum, tokens - turn)
    ).astype(jnp.bfloat16)
    grad_up = lax.dot_general(
        rotate_rows(x_rows, turn), pre_grad, (((0,), (0,)), ((), ())), preferred_element_type=jnp.float32
    ).astype(jnp.bfloat16)
    pos = lax.axis_index("r")
    pieces = [(pre_gather.block, pos)]
    for step in range(count - 1):
        up_piece, down_piece = pre_gather.ups[step], pre_gather.downs[step]
        up_at, down_at = pos - 1 - step, pos + 1 + step
        if 2 * step + 3 <= count:
            pieces += [(up_piece, up_at), (down_piece, down_at)]
        else:
            pieces.append((up_piece + down_piece, jnp.where(up_at >= 0, up_at, down_at)))
    sums = []
    for piece, at in pieces:
        back_rows = lax.dot_general(
            piece, up_tile, (((1,), (1,)), ((), ())), preferred_element_type=jnp.float32
        )
        sums.append((lax.psum_scatter(back_rows, "p", scatter_dimension=1, tiled=True), at))
    rows = pre_gather.block.shape[0]
    grad_blocks = out_grad.reshape(count, rows, out_grad.shape[1]).astype(jnp.float32)
    input_rows = []
    for k in range(count):
        total = grad_blocks[k]
        for value, at in sums:
            total = total + jnp.where(at == k, value, jnp.zeros_like(value))
        input_rows.append(total)
    input_grad = jnp.concatenate(input_rows, axis=0).astype(jnp.bfloat16)
    return (block_out, input_grad, grad_up[None], grad_down[None])


def solution(mesh):
    groups = mesh.shape["groups"]
    tile = mesh.shape["tile"]

    def run(hidden_in, w_up, w_down, out_grad):
        width_blocks = hidden_in.shape[1] // w_up.shape[1]
        grid = Mesh(
            np.asarray(mesh.devices).reshape(groups, width_blocks, tile // width_blocks),
            ("groups", "r", "p"),
        )
        cells = ("r", "p")
        return jax.shard_map(
            on_device,
            mesh=grid,
            in_specs=(
                P("groups", cells),
                P(cells, None, None),
                P(cells, None, None),
                P("groups", cells),
            ),
            out_specs=(
                P("groups", cells),
                P("groups", cells),
                P(cells, "groups", None),
                P(cells, "groups", None),
            ),
            check_vma=False,
        )(hidden_in, w_up, w_down, out_grad)

    return run
```

```python
import jax
import jax.numpy as jnp
import numpy as np
from jax import lax
from jax.sharding import Mesh
from jax.sharding import PartitionSpec as P


root_half = 0.7071067811865476
inv_root_tau = 0.3989422804014327


def gelu_value(values):
    return 0.5 * values * (1.0 + lax.erf(values * root_half))


def gelu_slope(values):
    return (
        0.5 * (1.0 + lax.erf(values * root_half))
        + values * jnp.exp(-0.5 * values * values) * inv_root_tau
    )


class LineReduce:
    def __init__(self, terms):
        self.count = lax.axis_size("r")
        self.pos = lax.axis_index("r")
        rows = terms.shape[0] // self.count
        self.shares = terms.reshape(self.count, rows, terms.shape[1])
        self.up_in = jnp.zeros((rows, terms.shape[1]), jnp.float32)
        self.down_in = jnp.zeros((rows, terms.shape[1]), jnp.float32)
        self.first = None

    def senders(self, step):
        return (0, step), (self.count - 1 - step, self.count - 1)

    def payload(self, step):
        if step == 0 and self.first is not None:
            return self.first
        last = self.count - 1
        up_block = jnp.clip(last - step + self.pos, 0, last)
        down_block = jnp.clip(self.pos + step - last, 0, last)
        up = self.up_in + lax.dynamic_index_in_dim(self.shares, up_block, 0, keepdims=False)
        down = self.down_in + lax.dynamic_index_in_dim(self.shares, down_block, 0, keepdims=False)
        return up.astype(jnp.bfloat16), down.astype(jnp.bfloat16)

    def receive(self, step, up, down):
        self.up_in = up.astype(jnp.float32)
        self.down_in = down.astype(jnp.float32)

    def result(self):
        own = lax.dynamic_index_in_dim(self.shares, self.pos, 0, keepdims=False)
        return self.up_in + own.astype(jnp.float32) + self.down_in


class LineGather:
    def __init__(self, block):
        self.count = lax.axis_size("r")
        self.pos = lax.axis_index("r")
        self.block = block
        self.up_cur = self.down_cur = block
        self.ups, self.downs = [], []

    def senders(self, step):
        return (step, self.count - 2), (1, self.count - 1 - step)

    def payload(self, step):
        return self.up_cur, self.down_cur

    def receive(self, step, up, down):
        self.up_cur, self.down_cur = up, down
        self.ups.append(up)
        self.downs.append(down)

    def result(self):
        count = self.count
        pieces = [self.block]
        for m in range(1, count):
            pieces.append(self.downs[m - 1] + self.ups[count - 1 - m])
        return jnp.concatenate(pieces, axis=0)


def rotate_rows(values, shift):
    doubled = jnp.concatenate([values, values], axis=0)
    return lax.dynamic_slice_in_dim(doubled, shift, values.shape[0], axis=0)


def run_slot(entries):
    pos = lax.axis_index("r")
    loads = [entry.payload(step) for entry, step in entries]
    ranges = [entry.senders(step) for entry, step in entries]
    received = []
    for direction, shift in ((0, 1), (1, -1)):
        combined = None
        pairs = []
        for load, rng in zip(loads, ranges):
            lo, hi = rng[direction]
            if lo > hi:
                continue
            pairs += [(i, i + shift) for i in range(lo, hi + 1)]
            mine = (pos >= lo) & (pos <= hi)
            combined = load[direction] if combined is None else jnp.where(mine, load[direction], combined)
        if combined is None:
            received.append(None)
            continue
        received.append(lax.ppermute(combined, "r", pairs))
    for (entry, step), load, rng in zip(entries, loads, ranges):
        parts = []
        for direction, shift in ((0, 1), (1, -1)):
            lo, hi = rng[direction]
            got = received[direction]
            if got is None or lo > hi:
                parts.append(jnp.zeros_like(load[direction]))
                continue
            mine = (pos >= lo + shift) & (pos <= hi + shift)
            parts.append(jnp.where(mine, got, jnp.zeros_like(got)))
        entry.receive(step, *parts)


def on_device(hidden_in, w_up, w_down, out_grad):
    up_tile = w_up[0]
    down_tile = w_down[0]
    count = lax.axis_size("r")
    x_rows = lax.all_gather(hidden_in, "p", axis=1, tiled=True)
    up_terms = jnp.dot(x_rows, up_tile, preferred_element_type=jnp.float32).astype(jnp.bfloat16)
    grad_rows = lax.all_gather(out_grad, "p", axis=1, tiled=True)
    grad_terms = lax.dot_general(
        grad_rows, down_tile, (((1,), (1,)), ((), ())), preferred_element_type=jnp.float32
    ).astype(jnp.bfloat16)

    up_sum = LineReduce(up_terms)
    if count > 1:
        rows = x_rows.shape[0] // count
        last = count - 1
        pos = lax.axis_index("r")

        own_rows = jnp.concatenate(
            [
                lax.dynamic_slice_in_dim(hidden_in, jnp.clip(last + pos, 0, last) * rows, rows, axis=0),
                lax.dynamic_slice_in_dim(hidden_in, jnp.clip(pos - last, 0, last) * rows, rows, axis=0),
            ],
            axis=0,
        )
        first_rows = lax.all_gather(own_rows, "p", axis=1, tiled=True)
        first = jnp.dot(first_rows, up_tile, preferred_element_type=jnp.float32).astype(jnp.bfloat16)
        up_sum.first = (first[:rows], first[rows:])
        run_slot([(up_sum, 0)])
        up_sum.up_in, up_sum.down_in, up_sum.shares = lax.optimization_barrier(
            (up_sum.up_in, up_sum.down_in, up_sum.shares)
        )
    for step in range(1, count - 1):
        run_slot([(up_sum, step)])
        if step == 1:
            up_sum.up_in, up_sum.down_in, grad_terms = lax.optimization_barrier(
                (up_sum.up_in, up_sum.down_in, grad_terms)
            )
    grad_sum = LineReduce(grad_terms)
    preact = up_sum.result()
    act_gather = LineGather(gelu_value(preact).astype(jnp.bfloat16))
    if count > 1:
        run_slot([(act_gather, 0)])
    slope = gelu_slope(preact)
    for step in range(1, count - 1):
        run_slot([(act_gather, step), (grad_sum, step - 1)])
        if step == 1:
            grad_sum.up_in, grad_sum.down_in, slope = lax.optimization_barrier(
                (grad_sum.up_in, grad_sum.down_in, slope)
            )
    tokens = x_rows.shape[0]
    turn = lax.axis_index("r") * (tokens // count)
    grad_turned = rotate_rows(grad_rows, turn)
    activation = act_gather.result()
    out_part = jnp.dot(activation, down_tile, preferred_element_type=jnp.float32)
    grad_down = lax.dot_general(
        activation, grad_turned, (((0,), (0,)), ((), ())), preferred_element_type=jnp.float32
    ).astype(jnp.bfloat16)
    if count > 1:
        run_slot([(grad_sum, count - 2)])
        grad_sum.up_in, grad_sum.down_in, out_part = lax.optimization_barrier(
            (grad_sum.up_in, grad_sum.down_in, out_part)
        )
    out_sum = lax.psum_scatter(out_part, "p", scatter_dimension=1, tiled=True)
    act_grad = grad_sum.result()
    pre_gather = LineGather((act_grad * slope).astype(jnp.bfloat16))
    for step in range(count - 1):
        run_slot([(pre_gather, step)])
        if step == min(1, count - 2):
            pre_gather.up_cur, pre_gather.down_cur, out_sum, grad_down = lax.optimization_barrier(
                (pre_gather.up_cur, pre_gather.down_cur, out_sum, grad_down)
            )
            pre_gather.ups[-1], pre_gather.downs[-1] = pre_gather.up_cur, pre_gather.down_cur
    pre_grad = pre_gather.result()
    block_out = (
        hidden_in.astype(jnp.float32) + rotate_rows(out_sum, tokens - turn)
    ).astype(jnp.bfloat16)
    grad_up = lax.dot_general(
        rotate_rows(x_rows, turn), pre_grad, (((0,), (0,)), ((), ())), preferred_element_type=jnp.float32
    ).astype(jnp.bfloat16)
    pos = lax.axis_index("r")
    pieces = [(pre_gather.block, pos)]
    for step in range(count - 1):
        up_piece, down_piece = pre_gather.ups[step], pre_gather.downs[step]
        up_at, down_at = pos - 1 - step, pos + 1 + step
        if 2 * step + 3 <= count:
            pieces += [(up_piece, up_at), (down_piece, down_at)]
        else:
            pieces.append((up_piece + down_piece, jnp.where(up_at >= 0, up_at, down_at)))
    sums = []
    for piece, at in pieces:
        back_rows = lax.dot_general(
            piece, up_tile, (((1,), (1,)), ((), ())), preferred_element_type=jnp.float32
        )
        sums.append((lax.psum_scatter(back_rows, "p", scatter_dimension=1, tiled=True), at))
    rows = pre_gather.block.shape[0]
    grad_blocks = out_grad.reshape(count, rows, out_grad.shape[1]).astype(jnp.float32)
    input_rows = []
    for k in range(count):
        total = grad_blocks[k]
        for value, at in sums:
            total = total + jnp.where(at == k, value, jnp.zeros_like(value))
        input_rows.append(total)
    input_grad = jnp.concatenate(input_rows, axis=0).astype(jnp.bfloat16)
    return (block_out, input_grad, grad_up[None], grad_down[None])


def solution(mesh):
    groups = mesh.shape["groups"]
    tile = mesh.shape["tile"]

    def run(hidden_in, w_up, w_down, out_grad):
        width_blocks = hidden_in.shape[1] // w_up.shape[1]
        grid = Mesh(
            np.asarray(mesh.devices).reshape(groups, width_blocks, tile // width_blocks),
            ("groups", "r", "p"),
        )
        cells = ("r", "p")
        return jax.shard_map(
            on_device,
            mesh=grid,
            in_specs=(
                P("groups", cells),
                P(cells, None, None),
                P(cells, None, None),
                P("groups", cells),
            ),
            out_specs=(
                P("groups", cells),
                P("groups", cells),
                P(cells, "groups", None),
                P(cells, "groups", None),
            ),
            check_vma=False,
        )(hidden_in, w_up, w_down, out_grad)

    return run
```

```python
import jax
import jax.numpy as jnp
import numpy as np
from jax import lax
from jax.sharding import Mesh
from jax.sharding import PartitionSpec as P


root_half = 0.7071067811865476
inv_root_tau = 0.3989422804014327


def gelu_value(values):
    return 0.5 * values * (1.0 + lax.erf(values * root_half))


def gelu_slope(values):
    return (
        0.5 * (1.0 + lax.erf(values * root_half))
        + values * jnp.exp(-0.5 * values * values) * inv_root_tau
    )


class LineReduce:
    def __init__(self, terms):
        self.count = lax.axis_size("r")
        self.pos = lax.axis_index("r")
        rows = terms.shape[0] // self.count
        self.shares = terms.reshape(self.count, rows, terms.shape[1])
        self.up_in = jnp.zeros((rows, terms.shape[1]), jnp.float32)
        self.down_in = jnp.zeros((rows, terms.shape[1]), jnp.float32)
        self.first = None

    def senders(self, step):
        return (0, step), (self.count - 1 - step, self.count - 1)

    def payload(self, step):
        if step == 0 and self.first is not None:
            return self.first
        last = self.count - 1
        up_block = jnp.clip(last - step + self.pos, 0, last)
        down_block = jnp.clip(self.pos + step - last, 0, last)
        up = self.up_in + lax.dynamic_index_in_dim(self.shares, up_block, 0, keepdims=False)
        down = self.down_in + lax.dynamic_index_in_dim(self.shares, down_block, 0, keepdims=False)
        return up.astype(jnp.bfloat16), down.astype(jnp.bfloat16)

    def receive(self, step, up, down):
        self.up_in = up.astype(jnp.float32)
        self.down_in = down.astype(jnp.float32)

    def result(self):
        own = lax.dynamic_index_in_dim(self.shares, self.pos, 0, keepdims=False)
        return self.up_in + own.astype(jnp.float32) + self.down_in


class LineGather:
    def __init__(self, block):
        self.count = lax.axis_size("r")
        self.pos = lax.axis_index("r")
        self.block = block
        self.up_cur = self.down_cur = block
        self.ups, self.downs = [], []

    def senders(self, step):
        return (step, self.count - 2), (1, self.count - 1 - step)

    def payload(self, step):
        return self.up_cur, self.down_cur

    def receive(self, step, up, down):
        self.up_cur, self.down_cur = up, down
        self.ups.append(up)
        self.downs.append(down)

    def result(self):
        count = self.count
        pieces = [self.block]
        for m in range(1, count):
            pieces.append(self.downs[m - 1] + self.ups[count - 1 - m])
        return jnp.concatenate(pieces, axis=0)


def rotate_rows(values, shift):
    doubled = jnp.concatenate([values, values], axis=0)
    return lax.dynamic_slice_in_dim(doubled, shift, values.shape[0], axis=0)


def run_slot(entries):
    pos = lax.axis_index("r")
    loads = [entry.payload(step) for entry, step in entries]
    ranges = [entry.senders(step) for entry, step in entries]
    received = []
    for direction, shift in ((0, 1), (1, -1)):
        combined = None
        pairs = []
        for load, rng in zip(loads, ranges):
            lo, hi = rng[direction]
            if lo > hi:
                continue
            pairs += [(i, i + shift) for i in range(lo, hi + 1)]
            mine = (pos >= lo) & (pos <= hi)
            combined = load[direction] if combined is None else jnp.where(mine, load[direction], combined)
        if combined is None:
            received.append(None)
            continue
        received.append(lax.ppermute(combined, "r", pairs))
    for (entry, step), load, rng in zip(entries, loads, ranges):
        parts = []
        for direction, shift in ((0, 1), (1, -1)):
            lo, hi = rng[direction]
            got = received[direction]
            if got is None or lo > hi:
                parts.append(jnp.zeros_like(load[direction]))
                continue
            mine = (pos >= lo + shift) & (pos <= hi + shift)
            parts.append(jnp.where(mine, got, jnp.zeros_like(got)))
        entry.receive(step, *parts)


def on_device(hidden_in, w_up, w_down, out_grad):
    up_tile = w_up[0]
    down_tile = w_down[0]
    count = lax.axis_size("r")
    x_rows = lax.all_gather(hidden_in, "p", axis=1, tiled=True)
    up_terms = jnp.dot(x_rows, up_tile, preferred_element_type=jnp.float32).astype(jnp.bfloat16)
    grad_rows = lax.all_gather(out_grad, "p", axis=1, tiled=True)
    grad_terms = lax.dot_general(
        grad_rows, down_tile, (((1,), (1,)), ((), ())), preferred_element_type=jnp.float32
    ).astype(jnp.bfloat16)

    up_sum = LineReduce(up_terms)
    if count > 1:
        rows = x_rows.shape[0] // count
        last = count - 1
        pos = lax.axis_index("r")

        first_rows = jnp.concatenate(
            [
                lax.dynamic_slice_in_dim(x_rows, jnp.clip(last + pos, 0, last) * rows, rows, axis=0),
                lax.dynamic_slice_in_dim(x_rows, jnp.clip(pos - last, 0, last) * rows, rows, axis=0),
            ],
            axis=0,
        )
        first = jnp.dot(first_rows, up_tile, preferred_element_type=jnp.float32).astype(jnp.bfloat16)
        up_sum.first = (first[:rows], first[rows:])
        run_slot([(up_sum, 0)])
        up_sum.up_in, up_sum.down_in, up_sum.shares = lax.optimization_barrier(
            (up_sum.up_in, up_sum.down_in, up_sum.shares)
        )
    for step in range(1, count - 1):
        run_slot([(up_sum, step)])
        if step == 1:
            up_sum.up_in, up_sum.down_in, grad_terms = lax.optimization_barrier(
                (up_sum.up_in, up_sum.down_in, grad_terms)
            )
    grad_sum = LineReduce(grad_terms)
    preact = up_sum.result()
    act_gather = LineGather(gelu_value(preact).astype(jnp.bfloat16))
    if count > 1:
        run_slot([(act_gather, 0)])
    slope = gelu_slope(preact)
    for step in range(1, count - 1):
        run_slot([(act_gather, step), (grad_sum, step - 1)])
        if step == 1:
            grad_sum.up_in, grad_sum.down_in, slope = lax.optimization_barrier(
                (grad_sum.up_in, grad_sum.down_in, slope)
            )
    tokens = x_rows.shape[0]
    turn = lax.axis_index("r") * (tokens // count)
    grad_turned = rotate_rows(grad_rows, turn)
    activation = act_gather.result()
    out_part = jnp.dot(activation, down_tile, preferred_element_type=jnp.float32)
    grad_down = lax.dot_general(
        activation, grad_turned, (((0,), (0,)), ((), ())), preferred_element_type=jnp.float32
    ).astype(jnp.bfloat16)
    if count > 1:
        run_slot([(grad_sum, count - 2)])
        grad_sum.up_in, grad_sum.down_in, out_part = lax.optimization_barrier(
            (grad_sum.up_in, grad_sum.down_in, out_part)
        )
    out_sum = lax.psum_scatter(out_part, "p", scatter_dimension=1, tiled=True)
    act_grad = grad_sum.result()
    pre_gather = LineGather((act_grad * slope).astype(jnp.bfloat16))
    for step in range(count - 1):
        run_slot([(pre_gather, step)])
        if step == min(1, count - 2):
            pre_gather.up_cur, pre_gather.down_cur, out_sum, grad_down = lax.optimization_barrier(
                (pre_gather.up_cur, pre_gather.down_cur, out_sum, grad_down)
            )
            pre_gather.ups[-1], pre_gather.downs[-1] = pre_gather.up_cur, pre_gather.down_cur
    pre_grad = pre_gather.result()
    block_out = (
        hidden_in.astype(jnp.float32) + rotate_rows(out_sum, tokens - turn)
    ).astype(jnp.bfloat16)
    grad_up = lax.dot_general(
        rotate_rows(x_rows, turn), pre_grad, (((0,), (0,)), ((), ())), preferred_element_type=jnp.float32
    ).astype(jnp.bfloat16)
    pos = lax.axis_index("r")
    pieces = [(pre_gather.block, pos)]
    for step in range(count - 1):
        up_piece, down_piece = pre_gather.ups[step], pre_gather.downs[step]
        up_at, down_at = pos - 1 - step, pos + 1 + step
        if 2 * step + 3 <= count:
            pieces += [(up_piece, up_at), (down_piece, down_at)]
        else:
            pieces.append((up_piece + down_piece, jnp.where(up_at >= 0, up_at, down_at)))
    sums = []
    for piece, at in pieces:
        back_rows = lax.dot_general(
            piece, up_tile, (((1,), (1,)), ((), ())), preferred_element_type=jnp.float32
        )
        sums.append((lax.psum_scatter(back_rows, "p", scatter_dimension=1, tiled=True), at))
    rows = pre_gather.block.shape[0]
    grad_blocks = out_grad.reshape(count, rows, out_grad.shape[1]).astype(jnp.float32)
    input_rows = []
    for k in range(count):
        total = grad_blocks[k]
        for value, at in sums:
            total = total + jnp.where(at == k, value, jnp.zeros_like(value))
        input_rows.append(total)
    input_grad = jnp.concatenate(input_rows, axis=0).astype(jnp.bfloat16)
    return (block_out, input_grad, grad_up[None], grad_down[None])


def solution(mesh):
    groups = mesh.shape["groups"]
    tile = mesh.shape["tile"]

    def run(hidden_in, w_up, w_down, out_grad):
        width_blocks = hidden_in.shape[1] // w_up.shape[1]
        grid = Mesh(
            np.asarray(mesh.devices).reshape(groups, width_blocks, tile // width_blocks),
            ("groups", "r", "p"),
        )
        cells = ("r", "p")
        return jax.shard_map(
            on_device,
            mesh=grid,
            in_specs=(
                P("groups", cells),
                P(cells, None, None),
                P(cells, None, None),
                P("groups", cells),
            ),
            out_specs=(
                P("groups", cells),
                P("groups", cells),
                P(cells, "groups", None),
                P(cells, "groups", None),
            ),
            check_vma=False,
        )(hidden_in, w_up, w_down, out_grad)

    return run
```

```python
import jax
import jax.numpy as jnp
import numpy as np
from jax import lax
from jax.sharding import Mesh
from jax.sharding import PartitionSpec as P


root_half = 0.7071067811865476
inv_root_tau = 0.3989422804014327


def gelu_value(values):
    return 0.5 * values * (1.0 + lax.erf(values * root_half))


def gelu_slope(values):
    return (
        0.5 * (1.0 + lax.erf(values * root_half))
        + values * jnp.exp(-0.5 * values * values) * inv_root_tau
    )


class LineReduce:
    def __init__(self, terms):
        self.count = lax.axis_size("r")
        self.pos = lax.axis_index("r")
        rows = terms.shape[0] // self.count
        self.shares = terms.reshape(self.count, rows, terms.shape[1])
        self.up_in = jnp.zeros((rows, terms.shape[1]), jnp.float32)
        self.down_in = jnp.zeros((rows, terms.shape[1]), jnp.float32)
        self.first = None

    def senders(self, step):
        return (0, step), (self.count - 1 - step, self.count - 1)

    def payload(self, step):
        if step == 0 and self.first is not None:
            return self.first
        last = self.count - 1
        up_block = jnp.clip(last - step + self.pos, 0, last)
        down_block = jnp.clip(self.pos + step - last, 0, last)
        up = self.up_in + lax.dynamic_index_in_dim(self.shares, up_block, 0, keepdims=False)
        down = self.down_in + lax.dynamic_index_in_dim(self.shares, down_block, 0, keepdims=False)
        return up.astype(jnp.bfloat16), down.astype(jnp.bfloat16)

    def receive(self, step, up, down):
        self.up_in = up.astype(jnp.float32)
        self.down_in = down.astype(jnp.float32)

    def result(self):
        own = lax.dynamic_index_in_dim(self.shares, self.pos, 0, keepdims=False)
        return self.up_in + own.astype(jnp.float32) + self.down_in


class LineGather:
    def __init__(self, block):
        self.count = lax.axis_size("r")
        self.pos = lax.axis_index("r")
        self.block = block
        self.up_cur = self.down_cur = block
        self.ups, self.downs = [], []

    def senders(self, step):
        return (step, self.count - 2), (1, self.count - 1 - step)

    def payload(self, step):
        return self.up_cur, self.down_cur

    def receive(self, step, up, down):
        self.up_cur, self.down_cur = up, down
        self.ups.append(up)
        self.downs.append(down)

    def result(self):
        count = self.count
        pieces = [self.block]
        for m in range(1, count):
            pieces.append(self.downs[m - 1] + self.ups[count - 1 - m])
        return jnp.concatenate(pieces, axis=0)


def rotate_rows(values, shift):
    doubled = jnp.concatenate([values, values], axis=0)
    return lax.dynamic_slice_in_dim(doubled, shift, values.shape[0], axis=0)


def run_slot(entries):
    pos = lax.axis_index("r")
    loads = [entry.payload(step) for entry, step in entries]
    ranges = [entry.senders(step) for entry, step in entries]
    received = []
    for direction, shift in ((0, 1), (1, -1)):
        combined = None
        pairs = []
        for load, rng in zip(loads, ranges):
            lo, hi = rng[direction]
            if lo > hi:
                continue
            pairs += [(i, i + shift) for i in range(lo, hi + 1)]
            mine = (pos >= lo) & (pos <= hi)
            combined = load[direction] if combined is None else jnp.where(mine, load[direction], combined)
        if combined is None:
            received.append(None)
            continue
        received.append(lax.ppermute(combined, "r", pairs))
    for (entry, step), load, rng in zip(entries, loads, ranges):
        parts = []
        for direction, shift in ((0, 1), (1, -1)):
            lo, hi = rng[direction]
            got = received[direction]
            if got is None or lo > hi:
                parts.append(jnp.zeros_like(load[direction]))
                continue
            mine = (pos >= lo + shift) & (pos <= hi + shift)
            parts.append(jnp.where(mine, got, jnp.zeros_like(got)))
        entry.receive(step, *parts)


def on_device(hidden_in, w_up, w_down, out_grad):
    up_tile = w_up[0]
    down_tile = w_down[0]
    count = lax.axis_size("r")
    x_rows = lax.all_gather(hidden_in, "p", axis=1, tiled=True)
    up_terms = jnp.dot(x_rows, up_tile, preferred_element_type=jnp.float32).astype(jnp.bfloat16)
    grad_rows = lax.all_gather(out_grad, "p", axis=1, tiled=True)
    grad_terms = lax.dot_general(
        grad_rows, down_tile, (((1,), (1,)), ((), ())), preferred_element_type=jnp.float32
    ).astype(jnp.bfloat16)

    up_sum = LineReduce(up_terms)
    if count > 1:
        rows = x_rows.shape[0] // count
        last = count - 1
        pos = lax.axis_index("r")

        own_rows = jnp.concatenate(
            [
                lax.dynamic_slice_in_dim(hidden_in, jnp.clip(last + pos, 0, last) * rows, rows, axis=0),
                lax.dynamic_slice_in_dim(hidden_in, jnp.clip(pos - last, 0, last) * rows, rows, axis=0),
            ],
            axis=0,
        )
        first_rows = lax.all_gather(own_rows, "p", axis=1, tiled=True)
        first = jnp.dot(first_rows, up_tile, preferred_element_type=jnp.float32).astype(jnp.bfloat16)
        up_sum.first = (first[:rows], first[rows:])
        run_slot([(up_sum, 0)])
        up_sum.up_in, up_sum.down_in, up_sum.shares = lax.optimization_barrier(
            (up_sum.up_in, up_sum.down_in, up_sum.shares)
        )
    for step in range(1, count - 1):
        run_slot([(up_sum, step)])
        if step == 1:
            up_sum.up_in, up_sum.down_in, grad_terms = lax.optimization_barrier(
                (up_sum.up_in, up_sum.down_in, grad_terms)
            )
    grad_sum = LineReduce(grad_terms)
    preact = up_sum.result()
    act_gather = LineGather(gelu_value(preact).astype(jnp.bfloat16))
    if count > 1:
        run_slot([(act_gather, 0)])
    slope = gelu_slope(preact)
    for step in range(1, count - 1):
        run_slot([(act_gather, step), (grad_sum, step - 1)])
    tokens = x_rows.shape[0]
    turn = lax.axis_index("r") * (tokens // count)
    grad_turned = rotate_rows(grad_rows, turn)
    activation = act_gather.result()
    out_part = jnp.dot(activation, down_tile, preferred_element_type=jnp.float32)
    grad_down = lax.dot_general(
        activation, grad_turned, (((0,), (0,)), ((), ())), preferred_element_type=jnp.float32
    ).astype(jnp.bfloat16)
    if count > 1:
        run_slot([(grad_sum, count - 2)])
        grad_sum.up_in, grad_sum.down_in, out_part = lax.optimization_barrier(
            (grad_sum.up_in, grad_sum.down_in, out_part)
        )
    out_sum = lax.psum_scatter(out_part, "p", scatter_dimension=1, tiled=True)
    act_grad = grad_sum.result()
    pre_gather = LineGather((act_grad * slope).astype(jnp.bfloat16))
    for step in range(count - 1):
        run_slot([(pre_gather, step)])
        if step == min(1, count - 2):
            pre_gather.up_cur, pre_gather.down_cur, out_sum, grad_down = lax.optimization_barrier(
                (pre_gather.up_cur, pre_gather.down_cur, out_sum, grad_down)
            )
            pre_gather.ups[-1], pre_gather.downs[-1] = pre_gather.up_cur, pre_gather.down_cur
    pre_grad = pre_gather.result()
    block_out = (
        hidden_in.astype(jnp.float32) + rotate_rows(out_sum, tokens - turn)
    ).astype(jnp.bfloat16)
    grad_up = lax.dot_general(
        rotate_rows(x_rows, turn), pre_grad, (((0,), (0,)), ((), ())), preferred_element_type=jnp.float32
    ).astype(jnp.bfloat16)
    pos = lax.axis_index("r")
    pieces = [(pre_gather.block, pos)]
    for step in range(count - 1):
        up_piece, down_piece = pre_gather.ups[step], pre_gather.downs[step]
        up_at, down_at = pos - 1 - step, pos + 1 + step
        if 2 * step + 3 <= count:
            pieces += [(up_piece, up_at), (down_piece, down_at)]
        else:
            pieces.append((up_piece + down_piece, jnp.where(up_at >= 0, up_at, down_at)))
    sums = []
    for piece, at in pieces:
        back_rows = lax.dot_general(
            piece, up_tile, (((1,), (1,)), ((), ())), preferred_element_type=jnp.float32
        )
        sums.append((lax.psum_scatter(back_rows, "p", scatter_dimension=1, tiled=True), at))
    rows = pre_gather.block.shape[0]
    grad_blocks = out_grad.reshape(count, rows, out_grad.shape[1]).astype(jnp.float32)
    input_rows = []
    for k in range(count):
        total = grad_blocks[k]
        for value, at in sums:
            total = total + jnp.where(at == k, value, jnp.zeros_like(value))
        input_rows.append(total)
    input_grad = jnp.concatenate(input_rows, axis=0).astype(jnp.bfloat16)
    return (block_out, input_grad, grad_up[None], grad_down[None])


def solution(mesh):
    groups = mesh.shape["groups"]
    tile = mesh.shape["tile"]

    def run(hidden_in, w_up, w_down, out_grad):
        width_blocks = hidden_in.shape[1] // w_up.shape[1]
        grid = Mesh(
            np.asarray(mesh.devices).reshape(groups, width_blocks, tile // width_blocks),
            ("groups", "r", "p"),
        )
        cells = ("r", "p")
        return jax.shard_map(
            on_device,
            mesh=grid,
            in_specs=(
                P("groups", cells),
                P(cells, None, None),
                P(cells, None, None),
                P("groups", cells),
            ),
            out_specs=(
                P("groups", cells),
                P("groups", cells),
                P(cells, "groups", None),
                P(cells, "groups", None),
            ),
            check_vma=False,
        )(hidden_in, w_up, w_down, out_grad)

    return run
```
